512 devices in a mesh: chan: 128 (over z, y, core), tm: 4 (over x).
Axes of the slice: x: 4, y: 8, z: 8, core: 2. Of those that a mesh axis runs over, the one named last changes fastest.
Arguments:
- visibilities: bfloat16 [4, 1024, 16384], P('tm', 'chan'), may hold values from -6 to 6
- flags: int32 [4, 1024, 2048], P('tm', 'chan'), may hold values 0 or 1
- taper: float32 [1024], P('chan'), may hold values from 0.3 to 1
- group_ids: int32 [2048], replicated, may hold values from 0 to 15
Outputs:
- spectrum: float32 [4, 16, 1024], P(None, None, 'chan')
The draws below stay inside these ranges and needn't reach their ends.
Inputs may be any that keep to these rules, and one draw needn't show every extreme that they name: `group_ids`: each baseline's group number.
All inputs are finite; a program needn't handle non-finite values. No bound on the sum of `flags` on one device may be relied on, other than what follows from the above.
Results may differ from the reference program's by a relative error of at most 0.0051.
Values may be sent and summed in bfloat16 or wider, within the bound.
No kernel may reach another device: no remote copies, remote signals or barrier semaphores. Data moves between devices by JAX's collectives and lax.ppermute only.
A program may use at most 64 MiB of HBM per device.

```python
import math
import jax
import jax.numpy as jnp
import numpy as np
from jax import lax

NCH = 1024
BL = 2048
G = 16
TIMES = 4


def with_ends(entries, key, smallest, largest):
    longest = entries.shape.index(max(entries.shape))
    spots = []
    for shift in (0, 1):
        where = [jax.random.randint(jax.random.fold_in(key, axis), (), 0, length) for axis, length in enumerate(entries.shape)]
        where[longest] = (where[longest] + shift) % entries.shape[longest]
        spots.append(tuple(where))
    return entries.at[spots[0]].set(smallest).at[spots[1]].set(largest)


def shard_levels(own_key, shape, cuts, smallest, top_value):
    level, own = 1.0, jax.random.fold_in(own_key, 6)
    for axis_at, parts in cuts:
        heights = jnp.exp(jax.random.uniform(jax.random.fold_in(own, axis_at), (parts,), jnp.float32, smallest / len(cuts), top_value / len(cuts)))
        level = level * jnp.repeat(heights, shape[axis_at] // parts).reshape([-1 if axis == axis_at else 1 for axis in range(len(shape))])
    return level


def rank_bounds(count, slope):
    loads = [(1 << 20) // math.isqrt(standing ** slope) + 1 for standing in range(1, count + 1)]
    spread = 1 + sum(loads) // (1 << 30)
    return np.cumsum(np.array([max(1, weight // spread) for weight in loads]))


def ranked(rng, extent, amount, skew):
    table = rank_bounds(amount, skew)
    pick = jax.random.randint(jax.random.fold_in(rng, 1), extent, 0, int(table[amount - 1]))
    standing = jnp.searchsorted(jnp.asarray(table, jnp.int32), pick, side="right")
    return jax.random.permutation(jax.random.fold_in(rng, 2), amount)[standing].astype(jnp.int32)


def normal_values(rng, dims, deviation, limit, split=(), kind=jnp.bfloat16):
    drawn = deviation * jax.random.normal(rng, dims, jnp.float32)
    if split:
        drawn = drawn * shard_levels(rng, dims, split, -0.22, 0.18)
    return jnp.clip(drawn, -limit, limit).astype(kind)


def setup_inputs(seed: int = 0) -> dict:
    arg_keys = jax.random.split(jax.random.key(seed), 5)
    return {
        "visibilities": normal_values(arg_keys[0], (TIMES, NCH, BL * 8), 1.0, 6.0, ((0, 4), (1, 128))),
        "flags": with_ends((jax.random.randint(arg_keys[1], (TIMES, NCH, BL), 0, 4) < 1).astype(jnp.int32), jax.random.fold_in(arg_keys[1], 1), 0, 1),
        "taper": jnp.clip(0.3 + 0.7 * jax.random.uniform(arg_keys[2], (NCH,), jnp.float32) ** shard_levels(arg_keys[2], (NCH,), ((0, 128),), -0.2, 0.2), 0.3, 1.0),
        "group_ids": with_ends(ranked(arg_keys[3], (BL,), G, 2), jax.random.fold_in(arg_keys[3], 3), 0, G - 1).astype(jnp.int32),
    }


def tables(length):
    positions = jnp.arange(length, dtype=jnp.int32)
    product = positions[:, None] * positions[None, :] % length
    phases = product.astype(jnp.float32) * (2.0 * math.pi / length)
    normalizing_scale = 1.0 / math.sqrt(length)
    return ((jnp.cos(phases) * normalizing_scale).astype(jnp.bfloat16), (jnp.sin(phases) * normalizing_scale).astype(jnp.bfloat16))

def reference(visibilities, flags, taper, group_ids):
    weight = (1 - flags).astype(jnp.float32) * taper[None, :, None]
    shaped = visibilities.reshape(TIMES, NCH, BL, 8).astype(jnp.float32)
    tapered = (shaped * weight[..., None]).astype(jnp.bfloat16).reshape(TIMES, NCH, BL * 8)
    cos_tab, sin_tab = tables(NCH)
    group_member = (group_ids[None, :] == jnp.arange(G, dtype=jnp.int32)[:, None]).astype(jnp.float32)

    def one_time(gathered_output):
        cosine_part = jnp.dot(cos_tab, gathered_output, preferred_element_type=jnp.float32).reshape(NCH, BL, 4, 2)
        sine_part = jnp.dot(sin_tab, gathered_output, preferred_element_type=jnp.float32).reshape(NCH, BL, 4, 2)
        real_part = cosine_part[..., 0] + sine_part[..., 1]
        imag_part = cosine_part[..., 1] - sine_part[..., 0]
        group_real = jnp.einsum('dbs,gb->sgd', real_part, group_member, precision=lax.Precision.HIGHEST)
        group_imag = jnp.einsum('dbs,gb->sgd', imag_part, group_member, precision=lax.Precision.HIGHEST)
        autocorrelation_terms = jnp.einsum('dbs,gb->sgd', real_part * real_part + imag_part * imag_part, group_member, precision=lax.Precision.HIGHEST)
        return group_real * group_real + group_imag * group_imag - autocorrelation_terms
    cross = lax.optimization_barrier(jnp.sum(lax.map(one_time, tapered), axis=0))
    counts = lax.optimization_barrier(jnp.sum(group_member, axis=1))
    pair_count = jnp.maximum(counts * (counts - 1.0), 1.0)
    return cross / jnp.sqrt(pair_count * TIMES)[None, :, None]
```

```python
import math

import jax
import jax.numpy as jnp
from jax import lax
from jax.sharding import PartitionSpec as P

G = 16
REDUCE_BY_ALL_TO_ALL = True


def tables(length, minor):
    major = length // minor
    d = jnp.arange(length, dtype=jnp.int32)
    c1 = jnp.arange(major, dtype=jnp.int32)
    c0 = jnp.arange(minor, dtype=jnp.int32)
    step = 2.0 * math.pi / length
    ka = (d[:, None] * (minor * c1)[None, :]) % length
    kb = (d[:, None] * c0[None, :]) % length
    pa = ka.astype(jnp.float32) * step
    pb = kb.astype(jnp.float32) * step
    ca, sa = jnp.cos(pa)[:, :, None], jnp.sin(pa)[:, :, None]
    cb, sb = jnp.cos(pb)[:, None, :], jnp.sin(pb)[:, None, :]
    scale = 1.0 / math.sqrt(length)
    cos_tab = ((ca * cb - sa * sb) * scale).astype(jnp.bfloat16).reshape(length, length)
    sin_tab = ((sa * cb + ca * sb) * scale).astype(jnp.bfloat16).reshape(length, length)
    return cos_tab, sin_tab


def hi_dot(a, b):
    return jnp.dot(a, b, precision=lax.Precision.HIGHEST, preferred_element_type=jnp.float32)


def body(visibilities, flags, taper, group_ids):
    _, local_chans, column_entries = visibilities.shape
    baselines = column_entries // 8
    n_chan = lax.axis_size("chan")
    channels = local_chans * n_chan
    shard_bl = baselines // n_chan
    shard_cols = shard_bl * 8
    times_all = lax.axis_size("tm")

    weight = (1 - flags[0]).astype(jnp.float32) * taper[:, None]
    shaped = visibilities[0].reshape(local_chans, baselines, 8).astype(jnp.float32)
    tapered = (shaped * weight[..., None]).astype(jnp.bfloat16)
    tapered = tapered.reshape(local_chans, n_chan, shard_cols).transpose(1, 0, 2)
    turned = lax.all_to_all(tapered, "chan", 0, 0, tiled=True)
    turned = turned.reshape(channels, shard_cols)

    cos_tab, sin_tab = tables(channels, 128)
    cos_part = jnp.dot(cos_tab, turned, preferred_element_type=jnp.float32)
    sin_part = jnp.dot(sin_tab, turned, preferred_element_type=jnp.float32)

    me = lax.axis_index("chan")
    shard_groups = lax.dynamic_slice_in_dim(group_ids, me * shard_bl, shard_bl)
    member = (shard_groups[:, None] == jnp.arange(G, dtype=jnp.int32)[None, :]).astype(jnp.float32)
    eye_s = jnp.eye(4, dtype=jnp.float32)
    eye_b = jnp.eye(shard_bl, dtype=jnp.float32)
    r_one = jnp.array([0.0, 1.0], jnp.float32)
    r_zero = 1.0 - r_one
    m_gs = member[:, None, None, :, None] * eye_s[None, :, None, None, :]
    m0 = (m_gs * r_zero[None, None, :, None, None]).reshape(shard_cols, G * 4)
    m1 = (m_gs * r_one[None, None, :, None, None]).reshape(shard_cols, G * 4)
    p_bs = eye_b[:, None, None, :, None] * eye_s[None, :, None, None, :]
    p0 = (p_bs * r_zero[None, None, :, None, None]).reshape(shard_cols, shard_bl * 4)
    p1 = (p_bs * r_one[None, None, :, None, None]).reshape(shard_cols, shard_bl * 4)
    m_pow = (member[:, None, :, None] * eye_s[None, :, None, :]).reshape(shard_bl * 4, G * 4)

    group_real = hi_dot(cos_part, m0) + hi_dot(sin_part, m1)
    group_imag = hi_dot(cos_part, m1) - hi_dot(sin_part, m0)
    real_part = hi_dot(cos_part, p0) + hi_dot(sin_part, p1)
    imag_part = hi_dot(cos_part, p1) - hi_dot(sin_part, p0)
    auto = hi_dot(real_part * real_part + imag_part * imag_part, m_pow)

    own_d = channels // n_chan
    terms = jnp.stack([group_real, group_imag, auto], axis=0)
    terms = terms.reshape(3, n_chan, own_d, G * 4).transpose(1, 0, 2, 3)
    if REDUCE_BY_ALL_TO_ALL:
        owned = jnp.sum(lax.all_to_all(terms, "chan", 0, 0, tiled=True), axis=0)
    else:
        owned = lax.psum_scatter(terms, "chan", scatter_dimension=0, tiled=True)[0]
    cross = owned[0] * owned[0] + owned[1] * owned[1] - owned[2]
    cross = lax.psum(cross, "tm")

    member_all = (group_ids[None, :] == jnp.arange(G, dtype=jnp.int32)[:, None]).astype(jnp.float32)
    counts = jnp.sum(member_all, axis=1)
    pair_count = jnp.maximum(counts * (counts - 1.0), 1.0)
    norm = jnp.sqrt(pair_count * times_all)
    spectrum = cross.reshape(own_d, G, 4).transpose(2, 1, 0)
    return spectrum / norm[None, :, None]


def solution(mesh):
    return jax.shard_map(
        body,
        mesh=mesh,
        in_specs=(P("tm", "chan", None), P("tm", "chan", None), P("chan"), P()),
        out_specs=P(None, None, "chan"),
        check_vma=False,
    )
```

```python
import math

import jax
import jax.numpy as jnp
from jax import lax
from jax.sharding import PartitionSpec as P

G = 16
REDUCE_BY_ALL_TO_ALL = True


def tables(length, minor):
    major = length // minor
    d = jnp.arange(length, dtype=jnp.int32)
    c1 = jnp.arange(major, dtype=jnp.int32)
    c0 = jnp.arange(minor, dtype=jnp.int32)
    step = 2.0 * math.pi / length
    ka = (d[:, None] * (minor * c1)[None, :]) % length
    kb = (d[:, None] * c0[None, :]) % length
    pa = ka.astype(jnp.float32) * step
    pb = kb.astype(jnp.float32) * step
    ca, sa = jnp.cos(pa)[:, :, None], jnp.sin(pa)[:, :, None]
    cb, sb = jnp.cos(pb)[:, None, :], jnp.sin(pb)[:, None, :]
    scale = 1.0 / math.sqrt(length)
    cos_tab = ((ca * cb - sa * sb) * scale).astype(jnp.bfloat16).reshape(length, length)
    sin_tab = ((sa * cb + ca * sb) * scale).astype(jnp.bfloat16).reshape(length, length)
    return cos_tab, sin_tab


def hi_dot(a, b):
    return jnp.dot(a, b, precision=lax.Precision.HIGHEST, preferred_element_type=jnp.float32)


def tm_sum(x, n):
    if n & (n - 1):
        return lax.psum(x, "tm")
    step = 1
    while step < n:
        pairs = [(i, i ^ step) for i in range(n)]
        x = x + lax.ppermute(x, "tm", pairs)
        step *= 2
    return x


def body(visibilities, flags, taper, group_ids):
    _, local_chans, column_entries = visibilities.shape
    baselines = column_entries // 8
    n_chan = lax.axis_size("chan")
    channels = local_chans * n_chan
    shard_bl = baselines // n_chan
    shard_cols = shard_bl * 8
    times_all = lax.axis_size("tm")

    keep = (1 - flags[0]).astype(jnp.bfloat16).reshape(local_chans, n_chan, shard_bl)
    spread = (jnp.arange(shard_cols, dtype=jnp.int32)[None, :] // 8
              == jnp.arange(shard_bl, dtype=jnp.int32)[:, None]).astype(jnp.bfloat16)
    keep_cols = jnp.einsum("cjb,bl->jcl", keep, spread, preferred_element_type=jnp.float32)
    shaped = visibilities[0].reshape(local_chans, n_chan, shard_cols).transpose(1, 0, 2)
    tapered = (shaped.astype(jnp.float32) * (keep_cols * taper[None, :, None])).astype(jnp.bfloat16)
    turned = lax.all_to_all(tapered, "chan", 0, 0, tiled=True)
    turned = turned.reshape(channels, shard_cols)

    cos_tab, sin_tab = tables(channels, 128)
    cos_part = jnp.dot(cos_tab, turned, preferred_element_type=jnp.float32)
    sin_part = jnp.dot(sin_tab, turned, preferred_element_type=jnp.float32)

    me = lax.axis_index("chan")
    shard_groups = lax.dynamic_slice_in_dim(group_ids, me * shard_bl, shard_bl)
    member = (shard_groups[:, None] == jnp.arange(G, dtype=jnp.int32)[None, :]).astype(jnp.float32)
    eye_s = jnp.eye(4, dtype=jnp.float32)
    eye_b = jnp.eye(shard_bl, dtype=jnp.float32)
    r_one = jnp.array([0.0, 1.0], jnp.float32)
    r_zero = 1.0 - r_one
    m_gs = member[:, None, None, :, None] * eye_s[None, :, None, None, :]
    m0 = (m_gs * r_zero[None, None, :, None, None]).reshape(shard_cols, G * 4)
    m1 = (m_gs * r_one[None, None, :, None, None]).reshape(shard_cols, G * 4)
    p_bs = eye_b[:, None, None, :, None] * eye_s[None, :, None, None, :]
    p0 = (p_bs * r_zero[None, None, :, None, None]).reshape(shard_cols, shard_bl * 4)
    p1 = (p_bs * r_one[None, None, :, None, None]).reshape(shard_cols, shard_bl * 4)
    m_pow = (member[:, None, :, None] * eye_s[None, :, None, :]).reshape(shard_bl * 4, G * 4)

    group_real = hi_dot(cos_part, m0) + hi_dot(sin_part, m1)
    group_imag = hi_dot(cos_part, m1) - hi_dot(sin_part, m0)
    real_part = hi_dot(cos_part, p0) + hi_dot(sin_part, p1)
    imag_part = hi_dot(cos_part, p1) - hi_dot(sin_part, p0)
    auto = hi_dot(real_part * real_part + imag_part * imag_part, m_pow)

    own_d = channels // n_chan
    terms = jnp.stack([group_real, group_imag, auto], axis=0)
    terms = terms.reshape(3, n_chan, own_d, G * 4).transpose(1, 0, 2, 3)
    if REDUCE_BY_ALL_TO_ALL:
        owned = jnp.sum(lax.all_to_all(terms, "chan", 0, 0, tiled=True), axis=0)
    else:
        owned = lax.psum_scatter(terms, "chan", scatter_dimension=0, tiled=True)[0]
    cross = owned[0] * owned[0] + owned[1] * owned[1] - owned[2]
    cross = tm_sum(cross, times_all)

    member_all = (group_ids[None, :] == jnp.arange(G, dtype=jnp.int32)[:, None]).astype(jnp.float32)
    counts = jnp.sum(member_all, axis=1)
    pair_count = jnp.maximum(counts * (counts - 1.0), 1.0)
    norm = jnp.sqrt(pair_count * times_all)
    spectrum = cross.reshape(own_d, G, 4).transpose(2, 1, 0)
    return spectrum / norm[None, :, None]


def solution(mesh):
    return jax.shard_map(
        body,
        mesh=mesh,
        in_specs=(P("tm", "chan", None), P("tm", "chan", None), P("chan"), P()),
        out_specs=P(None, None, "chan"),
        check_vma=False,
    )
```

```python
import math

import jax
import jax.numpy as jnp
from jax import lax
from jax.sharding import PartitionSpec as P

G = 16


def tables(length, minor):
    major = length // minor
    d = jnp.arange(length, dtype=jnp.int32)
    c1 = jnp.arange(major, dtype=jnp.int32)
    c0 = jnp.arange(minor, dtype=jnp.int32)
    step = 2.0 * math.pi / length
    ka = (d[:, None] * (minor * c1)[None, :]) % length
    kb = (d[:, None] * c0[None, :]) % length
    pa = ka.astype(jnp.float32) * step
    pb = kb.astype(jnp.float32) * step
    ca, sa = jnp.cos(pa)[:, :, None], jnp.sin(pa)[:, :, None]
    cb, sb = jnp.cos(pb)[:, None, :], jnp.sin(pb)[:, None, :]
    scale = 1.0 / math.sqrt(length)
    cos_tab = ((ca * cb - sa * sb) * scale).astype(jnp.bfloat16).reshape(length, length)
    sin_tab = ((sa * cb + ca * sb) * scale).astype(jnp.bfloat16).reshape(length, length)
    return cos_tab, sin_tab


def hi_dot(a, b):
    return jnp.dot(a, b, precision=lax.Precision.HIGHEST, preferred_element_type=jnp.float32)


def tm_sum(x, n):
    if n & (n - 1):
        return lax.psum(x, "tm")
    step = 1
    while step < n:
        pairs = [(i, i ^ step) for i in range(n)]
        x = x + lax.ppermute(x, "tm", pairs)
        step *= 2
    return x


def body(visibilities, flags, taper, group_ids):
    _, local_chans, column_entries = visibilities.shape
    baselines = column_entries // 8
    n_chan = lax.axis_size("chan")
    channels = local_chans * n_chan
    shard_bl = baselines // n_chan
    shard_cols = shard_bl * 8
    times_all = lax.axis_size("tm")

    keep = (1 - flags[0]).astype(jnp.bfloat16).reshape(local_chans, n_chan, shard_bl)
    spread = (jnp.arange(shard_cols, dtype=jnp.int32)[None, :] // 8
              == jnp.arange(shard_bl, dtype=jnp.int32)[:, None]).astype(jnp.bfloat16)
    keep_cols = jnp.einsum("cjb,bl->jcl", keep, spread, preferred_element_type=jnp.float32)
    shaped = visibilities[0].reshape(local_chans, n_chan, shard_cols).transpose(1, 0, 2)
    tapered = (shaped.astype(jnp.float32) * (keep_cols * taper[None, :, None])).astype(jnp.bfloat16)
    turned = lax.all_to_all(tapered, "chan", 0, 0, tiled=True)
    turned = turned.reshape(channels, shard_cols)

    cos_tab, sin_tab = tables(channels, 128)
    cos_part = jnp.dot(cos_tab, turned, preferred_element_type=jnp.float32)
    sin_part = jnp.dot(sin_tab, turned, preferred_element_type=jnp.float32)

    member_full = (group_ids[:, None] == jnp.arange(G, dtype=jnp.int32)[None, :]).astype(jnp.bfloat16)
    member_full = member_full.reshape(n_chan, shard_bl, G)
    sums = jnp.einsum("jcbk,jbg->cgk", tapered.reshape(n_chan, local_chans, shard_bl, 8), member_full,
                      preferred_element_type=jnp.float32)
    sums = sums.reshape(local_chans, G * 8).T
    column = lax.all_to_all(sums, "chan", 0, 0, tiled=True).reshape(channels)
    col_hi = column.astype(jnp.bfloat16)
    col_lo = (column - col_hi.astype(jnp.float32)).astype(jnp.bfloat16)
    col_parts = jnp.stack([col_hi, col_lo], axis=1)
    col_cos = jnp.sum(jnp.dot(cos_tab, col_parts, preferred_element_type=jnp.float32), axis=1)
    col_sin = jnp.sum(jnp.dot(sin_tab, col_parts, preferred_element_type=jnp.float32), axis=1)

    me = lax.axis_index("chan")
    shard_groups = lax.dynamic_slice_in_dim(group_ids, me * shard_bl, shard_bl)
    member = (shard_groups[:, None] == jnp.arange(G, dtype=jnp.int32)[None, :]).astype(jnp.float32)
    eye_s = jnp.eye(4, dtype=jnp.float32)
    eye_b = jnp.eye(shard_bl, dtype=jnp.float32)
    r_one = jnp.array([0.0, 1.0], jnp.float32)
    r_zero = 1.0 - r_one
    p_bs = eye_b[:, None, None, :, None] * eye_s[None, :, None, None, :]
    p0 = (p_bs * r_zero[None, None, :, None, None]).reshape(shard_cols, shard_bl * 4)
    p1 = (p_bs * r_one[None, None, :, None, None]).reshape(shard_cols, shard_bl * 4)
    m_pow = (member[:, None, :, None] * eye_s[None, :, None, :]).reshape(shard_bl * 4, G * 4)
    real_part = hi_dot(cos_part, p0) + hi_dot(sin_part, p1)
    imag_part = hi_dot(cos_part, p1) - hi_dot(sin_part, p0)
    auto = hi_dot(real_part * real_part + imag_part * imag_part, m_pow)

    own_d = channels // n_chan
    payload = jnp.concatenate([
        auto.reshape(n_chan, own_d * G * 4),
        col_cos.reshape(n_chan, own_d),
        col_sin.reshape(n_chan, own_d),
    ], axis=1)
    got = lax.all_to_all(payload, "chan", 0, 0, tiled=True)
    auto_own = jnp.sum(got[:, :own_d * G * 4], axis=0).reshape(own_d, G, 4)
    cs = got[:, own_d * G * 4:].reshape(G, 4, 2, 2, own_d)
    group_real = cs[:, :, 0, 0] + cs[:, :, 1, 1]
    group_imag = cs[:, :, 1, 0] - cs[:, :, 0, 1]
    cross = group_real * group_real + group_imag * group_imag - auto_own.transpose(1, 2, 0)
    cross = tm_sum(cross, times_all)

    member_all = (group_ids[None, :] == jnp.arange(G, dtype=jnp.int32)[:, None]).astype(jnp.float32)
    counts = jnp.sum(member_all, axis=1)
    pair_count = jnp.maximum(counts * (counts - 1.0), 1.0)
    norm = jnp.sqrt(pair_count * times_all)
    spectrum = cross.transpose(1, 0, 2)
    return spectrum / norm[None, :, None]


def solution(mesh):
    return jax.shard_map(
        body,
        mesh=mesh,
        in_specs=(P("tm", "chan", None), P("tm", "chan", None), P("chan"), P()),
        out_specs=P(None, None, "chan"),
        check_vma=False,
    )
```

```python
import math

import jax
import jax.numpy as jnp
from jax import lax
from jax.sharding import PartitionSpec as P

G = 16


def tables(length, minor):
    major = length // minor
    d = jnp.arange(length, dtype=jnp.int32)
    c1 = jnp.arange(major, dtype=jnp.int32)
    c0 = jnp.arange(minor, dtype=jnp.int32)
    step = 2.0 * math.pi / length
    ka = (d[:, None] * (minor * c1)[None, :]) % length
    kb = (d[:, None] * c0[None, :]) % length
    pa = ka.astype(jnp.float32) * step
    pb = kb.astype(jnp.float32) * step
    ca, sa = jnp.cos(pa)[:, :, None], jnp.sin(pa)[:, :, None]
    cb, sb = jnp.cos(pb)[:, None, :], jnp.sin(pb)[:, None, :]
    scale = 1.0 / math.sqrt(length)
    cos_tab = ((ca * cb - sa * sb) * scale).astype(jnp.bfloat16).reshape(length, length)
    sin_tab = ((sa * cb + ca * sb) * scale).astype(jnp.bfloat16).reshape(length, length)
    return cos_tab, sin_tab


def hi_dot(a, b):
    return jnp.dot(a, b, precision=lax.Precision.HIGHEST, preferred_element_type=jnp.float32)


def tm_sum(x, n):
    if n & (n - 1):
        return lax.psum(x, "tm")
    step = 1
    while step < n:
        pairs = [(i, i ^ step) for i in range(n)]
        x = x + lax.ppermute(x, "tm", pairs)
        step *= 2
    return x


def body(visibilities, flags, taper, group_ids):
    _, local_chans, column_entries = visibilities.shape
    baselines = column_entries // 8
    n_chan = lax.axis_size("chan")
    channels = local_chans * n_chan
    shard_bl = baselines // n_chan
    shard_cols = shard_bl * 8
    times_all = lax.axis_size("tm")

    keep = (1 - flags[0]).astype(jnp.bfloat16).reshape(local_chans, n_chan, shard_bl)
    spread = (jnp.arange(shard_cols, dtype=jnp.int32)[None, :] // 8
              == jnp.arange(shard_bl, dtype=jnp.int32)[:, None]).astype(jnp.bfloat16)
    keep_cols = jnp.einsum("cjb,bl->jcl", keep, spread, preferred_element_type=jnp.float32)
    shaped = visibilities[0].reshape(local_chans, n_chan, shard_cols).transpose(1, 0, 2)
    tapered = (shaped.astype(jnp.float32) * (keep_cols * taper[None, :, None])).astype(jnp.bfloat16)

    member_full = (group_ids[:, None] == jnp.arange(G, dtype=jnp.int32)[None, :]).astype(jnp.bfloat16)
    member_full = member_full.reshape(n_chan, shard_bl, G)
    sums = jnp.einsum("jcbk,jbg->cgk", tapered.reshape(n_chan, local_chans, shard_bl, 8), member_full,
                      preferred_element_type=jnp.float32)
    sums = sums.reshape(local_chans, G * 8).T
    sums_hi = lax.reduce_precision(sums, exponent_bits=8, mantissa_bits=7)
    sums_lo = sums - sums_hi
    block = local_chans * shard_cols
    pad = -(block + 2 * local_chans) % 128
    payload = jnp.concatenate([
        tapered.reshape(n_chan, block),
        sums_hi.astype(jnp.bfloat16),
        sums_lo.astype(jnp.bfloat16),
        jnp.zeros((n_chan, pad), jnp.bfloat16),
    ], axis=1)
    got = lax.all_to_all(payload.reshape(n_chan, 1, -1), "chan", 0, 0, tiled=True).reshape(n_chan, -1)
    turned = got[:, :block].reshape(channels, shard_cols)
    col_parts = got[:, block:block + 2 * local_chans].reshape(n_chan, 2, local_chans)
    col_parts = col_parts.transpose(0, 2, 1).reshape(channels, 2)

    cos_tab, sin_tab = tables(channels, 128)
    cos_part = jnp.dot(cos_tab, turned, preferred_element_type=jnp.float32)
    sin_part = jnp.dot(sin_tab, turned, preferred_element_type=jnp.float32)
    col_cos = jnp.sum(jnp.dot(cos_tab, col_parts, preferred_element_type=jnp.float32), axis=1)
    col_sin = jnp.sum(jnp.dot(sin_tab, col_parts, preferred_element_type=jnp.float32), axis=1)

    me = lax.axis_index("chan")
    shard_groups = lax.dynamic_slice_in_dim(group_ids, me * shard_bl, shard_bl)
    member = (shard_groups[:, None] == jnp.arange(G, dtype=jnp.int32)[None, :]).astype(jnp.float32)
    eye_s = jnp.eye(4, dtype=jnp.float32)
    eye_b = jnp.eye(shard_bl, dtype=jnp.float32)
    r_one = jnp.array([0.0, 1.0], jnp.float32)
    r_zero = 1.0 - r_one
    p_bs = eye_b[:, None, None, :, None] * eye_s[None, :, None, None, :]
    p0 = (p_bs * r_zero[None, None, :, None, None]).reshape(shard_cols, shard_bl * 4)
    p1 = (p_bs * r_one[None, None, :, None, None]).reshape(shard_cols, shard_bl * 4)
    m_pow = (member[:, None, :, None] * eye_s[None, :, None, :]).reshape(shard_bl * 4, G * 4)
    real_part = hi_dot(cos_part, p0) + hi_dot(sin_part, p1)
    imag_part = hi_dot(cos_part, p1) - hi_dot(sin_part, p0)
    auto = hi_dot(real_part * real_part + imag_part * imag_part, m_pow)

    own_d = channels // n_chan
    payload = jnp.concatenate([
        auto.reshape(n_chan, own_d * G * 4),
        col_cos.reshape(n_chan, own_d),
        col_sin.reshape(n_chan, own_d),
    ], axis=1)
    got = lax.all_to_all(payload, "chan", 0, 0, tiled=True)
    auto_own = jnp.sum(got[:, :own_d * G * 4], axis=0).reshape(own_d, G, 4)
    cs = got[:, own_d * G * 4:].reshape(G, 4, 2, 2, own_d)
    group_real = cs[:, :, 0, 0] + cs[:, :, 1, 1]
    group_imag = cs[:, :, 1, 0] - cs[:, :, 0, 1]
    cross = group_real * group_real + group_imag * group_imag - auto_own.transpose(1, 2, 0)
    cross = tm_sum(cross, times_all)

    member_all = (group_ids[None, :] == jnp.arange(G, dtype=jnp.int32)[:, None]).astype(jnp.float32)
    counts = jnp.sum(member_all, axis=1)
    pair_count = jnp.maximum(counts * (counts - 1.0), 1.0)
    norm = jnp.sqrt(pair_count * times_all)
    spectrum = cross.transpose(1, 0, 2)
    return spectrum / norm[None, :, None]


def solution(mesh):
    return jax.shard_map(
        body,
        mesh=mesh,
        in_specs=(P("tm", "chan", None), P("tm", "chan", None), P("chan"), P()),
        out_specs=P(None, None, "chan"),
        check_vma=False,
    )
```

```python
import math

import jax
import jax.numpy as jnp
from jax import lax
from jax.sharding import PartitionSpec as P

G = 16


def tables(length, minor):
    major = length // minor
    d = jnp.arange(length, dtype=jnp.int32)
    c1 = jnp.arange(major, dtype=jnp.int32)
    c0 = jnp.arange(minor, dtype=jnp.int32)
    step = 2.0 * math.pi / length
    ka = (d[:, None] * (minor * c1)[None, :]) % length
    kb = (d[:, None] * c0[None, :]) % length
    pa = ka.astype(jnp.float32) * step
    pb = kb.astype(jnp.float32) * step
    ca, sa = jnp.cos(pa)[:, :, None], jnp.sin(pa)[:, :, None]
    cb, sb = jnp.cos(pb)[:, None, :], jnp.sin(pb)[:, None, :]
    scale = 1.0 / math.sqrt(length)
    cos_tab = ((ca * cb - sa * sb) * scale).astype(jnp.bfloat16).reshape(length, length)
    sin_tab = ((sa * cb + ca * sb) * scale).astype(jnp.bfloat16).reshape(length, length)
    return cos_tab, sin_tab


def hi_dot(a, b):
    return jnp.dot(a, b, precision=lax.Precision.HIGHEST, preferred_element_type=jnp.float32)


def tm_sum(x, n):
    if n & (n - 1):
        return lax.psum(x, "tm")
    step = 1
    while step < n:
        pairs = [(i, i ^ step) for i in range(n)]
        x = x + lax.ppermute(x, "tm", pairs)
        step *= 2
    return x


def body(visibilities, flags, taper, group_ids):
    _, local_chans, column_entries = visibilities.shape
    baselines = column_entries // 8
    n_chan = lax.axis_size("chan")
    channels = local_chans * n_chan
    shard_bl = baselines // n_chan
    shard_cols = shard_bl * 8
    times_all = lax.axis_size("tm")

    keep = (1 - flags[0]).astype(jnp.bfloat16).reshape(local_chans, n_chan, shard_bl)
    spread = (jnp.arange(shard_cols, dtype=jnp.int32)[None, :] // 8
              == jnp.arange(shard_bl, dtype=jnp.int32)[:, None]).astype(jnp.bfloat16)
    keep_cols = jnp.einsum("cjb,bl->jcl", keep, spread, preferred_element_type=jnp.float32)
    shaped = visibilities[0].reshape(local_chans, n_chan, shard_cols).transpose(1, 0, 2)
    tapered = (shaped.astype(jnp.float32) * (keep_cols * taper[None, :, None])).astype(jnp.bfloat16)

    member_full = (group_ids[:, None] == jnp.arange(G, dtype=jnp.int32)[None, :]).astype(jnp.bfloat16)
    member_full = member_full.reshape(n_chan, shard_bl, G)
    sums = jnp.einsum("jcbk,jbg->cgk", tapered.reshape(n_chan, local_chans, shard_bl, 8), member_full,
                      preferred_element_type=jnp.float32)
    sums = sums.reshape(local_chans, G * 8).T
    sums_hi = lax.reduce_precision(sums, exponent_bits=8, mantissa_bits=7)
    sums_lo = sums - sums_hi
    block = local_chans * shard_cols
    pad = -(block + 2 * local_chans) % 128
    payload = jnp.concatenate([
        tapered.reshape(n_chan, block),
        sums_hi.astype(jnp.bfloat16),
        sums_lo.astype(jnp.bfloat16),
        jnp.zeros((n_chan, pad), jnp.bfloat16),
    ], axis=1)
    got = lax.all_to_all(payload.reshape(n_chan, 1, -1), "chan", 0, 0, tiled=True).reshape(n_chan, -1)
    turned = got[:, :block].reshape(channels, shard_cols)
    col_parts = got[:, block:block + 2 * local_chans].reshape(n_chan, 2, local_chans)
    col_parts = col_parts.transpose(0, 2, 1).reshape(channels, 2)

    cols = jnp.arange(shard_cols, dtype=jnp.int32)
    target = (cols % 2) * (shard_cols // 2) + cols // 2
    permute = (target[:, None] == cols[None, :]).astype(jnp.bfloat16)
    turned = jnp.dot(turned, permute, preferred_element_type=jnp.float32).astype(jnp.bfloat16)
    cos_tab, sin_tab = tables(channels, 128)
    cos_part = jnp.dot(cos_tab, turned, preferred_element_type=jnp.float32)
    sin_part = jnp.dot(sin_tab, turned, preferred_element_type=jnp.float32)
    col_cos = jnp.sum(jnp.dot(cos_tab, col_parts, preferred_element_type=jnp.float32), axis=1)
    col_sin = jnp.sum(jnp.dot(sin_tab, col_parts, preferred_element_type=jnp.float32), axis=1)

    me = lax.axis_index("chan")
    shard_groups = lax.dynamic_slice_in_dim(group_ids, me * shard_bl, shard_bl)
    member = (shard_groups[:, None] == jnp.arange(G, dtype=jnp.int32)[None, :]).astype(jnp.float32)
    eye_s = jnp.eye(4, dtype=jnp.float32)
    m_pow = (member[:, None, :, None] * eye_s[None, :, None, :]).reshape(shard_bl * 4, G * 4)
    half = shard_cols // 2
    real_part = cos_part[:, :half] + sin_part[:, half:]
    imag_part = cos_part[:, half:] - sin_part[:, :half]
    auto = hi_dot(real_part * real_part + imag_part * imag_part, m_pow)

    own_d = channels // n_chan
    payload = jnp.concatenate([
        auto.reshape(n_chan, own_d * G * 4),
        col_cos.reshape(n_chan, own_d),
        col_sin.reshape(n_chan, own_d),
    ], axis=1)
    got = lax.all_to_all(payload, "chan", 0, 0, tiled=True)
    auto_own = jnp.sum(got[:, :own_d * G * 4], axis=0).reshape(own_d, G, 4)
    cs = got[:, own_d * G * 4:].reshape(G, 4, 2, 2, own_d)
    group_real = cs[:, :, 0, 0] + cs[:, :, 1, 1]
    group_imag = cs[:, :, 1, 0] - cs[:, :, 0, 1]
    cross = group_real * group_real + group_imag * group_imag - auto_own.transpose(1, 2, 0)
    cross = tm_sum(cross, times_all)

    member_all = (group_ids[None, :] == jnp.arange(G, dtype=jnp.int32)[:, None]).astype(jnp.float32)
    counts = jnp.sum(member_all, axis=1)
    pair_count = jnp.maximum(counts * (counts - 1.0), 1.0)
    norm = jnp.sqrt(pair_count * times_all)
    spectrum = cross.transpose(1, 0, 2)
    return spectrum / norm[None, :, None]


def solution(mesh):
    return jax.shard_map(
        body,
        mesh=mesh,
        in_specs=(P("tm", "chan", None), P("tm", "chan", None), P("chan"), P()),
        out_specs=P(None, None, "chan"),
        check_vma=False,
    )
```

```python
import math

import jax
import jax.numpy as jnp
from jax import lax
from jax.sharding import PartitionSpec as P

G = 16


def tables(length, minor):
    major = length // minor
    d = jnp.arange(length, dtype=jnp.int32)
    c1 = jnp.arange(major, dtype=jnp.int32)
    c0 = jnp.arange(minor, dtype=jnp.int32)
    step = 2.0 * math.pi / length
    ka = (d[:, None] * (minor * c1)[None, :]) % length
    kb = (d[:, None] * c0[None, :]) % length
    pa = ka.astype(jnp.float32) * step
    pb = kb.astype(jnp.float32) * step
    ca, sa = jnp.cos(pa)[:, :, None], jnp.sin(pa)[:, :, None]
    cb, sb = jnp.cos(pb)[:, None, :], jnp.sin(pb)[:, None, :]
    scale = 1.0 / math.sqrt(length)
    cos_tab = ((ca * cb - sa * sb) * scale).astype(jnp.bfloat16).reshape(length, length)
    sin_tab = ((sa * cb + ca * sb) * scale).astype(jnp.bfloat16).reshape(length, length)
    return cos_tab, sin_tab


def tm_sum(x, n):
    me = lax.axis_index("tm")
    got = [x] + [lax.ppermute(x, "tm", [(i, (i + k) % n) for i in range(n)]) for k in range(1, n)]
    got = jnp.stack(got)
    ordered = jnp.take(got, (me - jnp.arange(n)) % n, axis=0)
    while ordered.shape[0] > 1:
        if ordered.shape[0] % 2:
            ordered = jnp.concatenate([ordered[:1] + ordered[1:2], ordered[2:]])
        else:
            ordered = ordered[0::2] + ordered[1::2]
    return ordered[0]


def split_dot(a, b):
    hi = lax.reduce_precision(a, exponent_bits=8, mantissa_bits=7)
    lo = a - hi
    b16 = b.astype(jnp.bfloat16)
    return (jnp.dot(hi.astype(jnp.bfloat16), b16, preferred_element_type=jnp.float32)
            + jnp.dot(lo.astype(jnp.bfloat16), b16, preferred_element_type=jnp.float32))


def body(visibilities, flags, taper, group_ids):
    _, local_chans, column_entries = visibilities.shape
    baselines = column_entries // 8
    n_chan = lax.axis_size("chan")
    channels = local_chans * n_chan
    shard_bl = baselines // n_chan
    shard_cols = shard_bl * 8
    times_all = lax.axis_size("tm")

    keep = (1 - flags[0]).astype(jnp.bfloat16).reshape(local_chans, n_chan, shard_bl)
    spread = (jnp.arange(shard_cols, dtype=jnp.int32)[None, :] // 8
              == jnp.arange(shard_bl, dtype=jnp.int32)[:, None]).astype(jnp.bfloat16)
    keep_cols = jnp.einsum("cjb,bl->jcl", keep, spread, preferred_element_type=jnp.float32)
    shaped = visibilities[0].reshape(local_chans, n_chan, shard_cols).transpose(1, 0, 2)
    tapered = (shaped.astype(jnp.float32) * (keep_cols * taper[None, :, None])).astype(jnp.bfloat16)

    member_full = (group_ids[:, None] == jnp.arange(G, dtype=jnp.int32)[None, :]).astype(jnp.bfloat16)
    member_full = member_full.reshape(n_chan, shard_bl, G)
    sums = jnp.einsum("jcbk,jbg->cgk", tapered.reshape(n_chan, local_chans, shard_bl, 8), member_full,
                      preferred_element_type=jnp.float32)
    sums = sums.reshape(local_chans, G * 8).T
    sums_hi = lax.reduce_precision(sums, exponent_bits=8, mantissa_bits=7)
    sums_lo = sums - sums_hi
    block = local_chans * shard_cols
    pad = -(block + 2 * local_chans) % 128
    payload = jnp.concatenate([
        tapered.reshape(n_chan, block),
        sums_hi.astype(jnp.bfloat16),
        sums_lo.astype(jnp.bfloat16),
        jnp.zeros((n_chan, pad), jnp.bfloat16),
    ], axis=1)
    got = lax.all_to_all(payload.reshape(n_chan, 1, -1), "chan", 0, 0, tiled=True).reshape(n_chan, -1)
    turned = got[:, :block].reshape(channels, shard_cols)
    col_parts = got[:, block:block + 2 * local_chans].reshape(n_chan, 2, local_chans)
    col_parts = col_parts.transpose(0, 2, 1).reshape(channels, 2)

    cols = jnp.arange(shard_cols, dtype=jnp.int32)
    target = (cols % 2) * (shard_cols // 2) + cols // 2
    permute = (target[:, None] == cols[None, :]).astype(jnp.bfloat16)
    turned = jnp.dot(turned, permute, preferred_element_type=jnp.float32).astype(jnp.bfloat16)
    cos_tab, sin_tab = tables(channels, 128)
    cos_part = jnp.dot(cos_tab, turned, preferred_element_type=jnp.float32)
    sin_part = jnp.dot(sin_tab, turned, preferred_element_type=jnp.float32)
    col_cos = jnp.sum(jnp.dot(cos_tab, col_parts, preferred_element_type=jnp.float32), axis=1)
    col_sin = jnp.sum(jnp.dot(sin_tab, col_parts, preferred_element_type=jnp.float32), axis=1)

    me = lax.axis_index("chan")
    shard_groups = lax.dynamic_slice_in_dim(group_ids, me * shard_bl, shard_bl)
    member = (shard_groups[:, None] == jnp.arange(G, dtype=jnp.int32)[None, :]).astype(jnp.float32)
    eye_s = jnp.eye(4, dtype=jnp.float32)
    m_pow = (member[:, None, :, None] * eye_s[None, :, None, :]).reshape(shard_bl * 4, G * 4)
    half = shard_cols // 2
    real_part = cos_part[:, :half] + sin_part[:, half:]
    imag_part = cos_part[:, half:] - sin_part[:, :half]
    auto = split_dot(real_part * real_part + imag_part * imag_part, m_pow)

    own_d = channels // n_chan
    payload = jnp.concatenate([
        auto.reshape(n_chan, own_d * G * 4),
        col_cos.reshape(n_chan, own_d),
        col_sin.reshape(n_chan, own_d),
    ], axis=1)
    got = lax.all_to_all(payload, "chan", 0, 0, tiled=True)
    auto_own = jnp.sum(got[:, :own_d * G * 4], axis=0).reshape(own_d, G, 4)
    cs = got[:, own_d * G * 4:].reshape(G, 4, 2, 2, own_d)
    group_real = cs[:, :, 0, 0] + cs[:, :, 1, 1]
    group_imag = cs[:, :, 1, 0] - cs[:, :, 0, 1]
    cross = group_real * group_real + group_imag * group_imag - auto_own.transpose(1, 2, 0)
    cross = tm_sum(cross, times_all)

    member_all = (group_ids[None, :] == jnp.arange(G, dtype=jnp.int32)[:, None]).astype(jnp.float32)
    counts = jnp.sum(member_all, axis=1)
    pair_count = jnp.maximum(counts * (counts - 1.0), 1.0)
    norm = jnp.sqrt(pair_count * times_all)
    spectrum = cross.transpose(1, 0, 2)
    return spectrum / norm[None, :, None]


def solution(mesh):
    return jax.shard_map(
        body,
        mesh=mesh,
        in_specs=(P("tm", "chan", None), P("tm", "chan", None), P("chan"), P()),
        out_specs=P(None, None, "chan"),
        check_vma=False,
    )
```

```python
import math

import jax
import jax.numpy as jnp
from jax import lax
from jax.sharding import PartitionSpec as P

G = 16


def tables(length, minor):
    major = length // minor
    d = jnp.arange(length, dtype=jnp.int32)
    c1 = jnp.arange(major, dtype=jnp.int32)
    c0 = jnp.arange(minor, dtype=jnp.int32)
    step = 2.0 * math.pi / length
    ka = (d[:, None] * (minor * c1)[None, :]) % length
    kb = (d[:, None] * c0[None, :]) % length
    pa = ka.astype(jnp.float32) * step
    pb = kb.astype(jnp.float32) * step
    ca, sa = jnp.cos(pa)[:, :, None], jnp.sin(pa)[:, :, None]
    cb, sb = jnp.cos(pb)[:, None, :], jnp.sin(pb)[:, None, :]
    scale = 1.0 / math.sqrt(length)
    cos_tab = ((ca * cb - sa * sb) * scale).astype(jnp.bfloat16).reshape(length, length)
    sin_tab = ((sa * cb + ca * sb) * scale).astype(jnp.bfloat16).reshape(length, length)
    return cos_tab, sin_tab


def tm_sum(x, n):
    if n & (n - 1):
        return lax.psum(x, "tm")
    step = 1
    while step < n:
        pairs = [(i, i ^ step) for i in range(n)]
        x = x + lax.ppermute(x, "tm", pairs)
        step *= 2
    return x


def split_dot(a, b):
    hi = lax.reduce_precision(a, exponent_bits=8, mantissa_bits=7)
    lo = a - hi
    b16 = b.astype(jnp.bfloat16)
    return (jnp.dot(hi.astype(jnp.bfloat16), b16, preferred_element_type=jnp.float32)
            + jnp.dot(lo.astype(jnp.bfloat16), b16, preferred_element_type=jnp.float32))


def body(visibilities, flags, taper, group_ids):
    _, local_chans, column_entries = visibilities.shape
    baselines = column_entries // 8
    n_chan = lax.axis_size("chan")
    channels = local_chans * n_chan
    shard_bl = baselines // n_chan
    shard_cols = shard_bl * 8
    times_all = lax.axis_size("tm")

    keep = (1 - flags[0]).astype(jnp.bfloat16).reshape(local_chans, n_chan, shard_bl)
    spread = (jnp.arange(shard_cols, dtype=jnp.int32)[None, :] // 8
              == jnp.arange(shard_bl, dtype=jnp.int32)[:, None]).astype(jnp.bfloat16)
    keep_cols = jnp.einsum("cjb,bl->jcl", keep, spread, preferred_element_type=jnp.float32)
    shaped = visibilities[0].reshape(local_chans, n_chan, shard_cols).transpose(1, 0, 2)
    tapered = (shaped.astype(jnp.float32) * (keep_cols * taper[None, :, None])).astype(jnp.bfloat16)

    member_full = (group_ids[:, None] == jnp.arange(G, dtype=jnp.int32)[None, :]).astype(jnp.bfloat16)
    member_full = member_full.reshape(n_chan, shard_bl, G)
    sums = jnp.einsum("jcbk,jbg->cgk", tapered.reshape(n_chan, local_chans, shard_bl, 8), member_full,
                      preferred_element_type=jnp.float32)
    sums = sums.reshape(local_chans, G * 8).T
    sums_hi = lax.reduce_precision(sums, exponent_bits=8, mantissa_bits=7)
    sums_lo = sums - sums_hi
    block = local_chans * shard_cols
    pad = -(block + 2 * local_chans) % 128
    payload = jnp.concatenate([
        tapered.reshape(n_chan, block),
        sums_hi.astype(jnp.bfloat16),
        sums_lo.astype(jnp.bfloat16),
        jnp.zeros((n_chan, pad), jnp.bfloat16),
    ], axis=1)
    got = lax.all_to_all(payload.reshape(n_chan, 1, -1), "chan", 0, 0, tiled=True).reshape(n_chan, -1)
    turned = got[:, :block].reshape(channels, shard_cols)
    col_parts = got[:, block:block + 2 * local_chans].reshape(n_chan, 2, local_chans)
    col_parts = col_parts.transpose(0, 2, 1).reshape(channels, 2)

    cols = jnp.arange(shard_cols, dtype=jnp.int32)
    target = (cols % 2) * (shard_cols // 2) + cols // 2
    permute = (target[:, None] == cols[None, :]).astype(jnp.bfloat16)
    turned = jnp.dot(turned, permute, preferred_element_type=jnp.float32).astype(jnp.bfloat16)
    extra = 128 - col_parts.shape[1]
    rhs = jnp.concatenate([turned, col_parts, jnp.zeros((channels, extra), jnp.bfloat16)], axis=1)
    cos_tab, sin_tab = tables(channels, 128)
    cos_all = jnp.dot(cos_tab, rhs, preferred_element_type=jnp.float32)
    sin_all = jnp.dot(sin_tab, rhs, preferred_element_type=jnp.float32)
    cos_part, sin_part = cos_all[:, :shard_cols], sin_all[:, :shard_cols]
    col_cos = cos_all[:, shard_cols] + cos_all[:, shard_cols + 1]
    col_sin = sin_all[:, shard_cols] + sin_all[:, shard_cols + 1]

    me = lax.axis_index("chan")
    shard_groups = lax.dynamic_slice_in_dim(group_ids, me * shard_bl, shard_bl)
    member = (shard_groups[:, None] == jnp.arange(G, dtype=jnp.int32)[None, :]).astype(jnp.float32)
    eye_s = jnp.eye(4, dtype=jnp.float32)
    m_pow = (member[:, None, :, None] * eye_s[None, :, None, :]).reshape(shard_bl * 4, G * 4)
    half = shard_cols // 2
    real_part = cos_part[:, :half] + sin_part[:, half:]
    imag_part = cos_part[:, half:] - sin_part[:, :half]
    auto = split_dot(real_part * real_part + imag_part * imag_part, m_pow)

    own_d = channels // n_chan
    payload = jnp.concatenate([
        auto.reshape(n_chan, own_d * G * 4),
        col_cos.reshape(n_chan, own_d),
        col_sin.reshape(n_chan, own_d),
    ], axis=1)
    got = lax.all_to_all(payload, "chan", 0, 0, tiled=True)
    auto_own = jnp.sum(got[:, :own_d * G * 4], axis=0).reshape(own_d, G, 4)
    cs = got[:, own_d * G * 4:].reshape(G, 4, 2, 2, own_d)
    group_real = cs[:, :, 0, 0] + cs[:, :, 1, 1]
    group_imag = cs[:, :, 1, 0] - cs[:, :, 0, 1]
    cross = group_real * group_real + group_imag * group_imag - auto_own.transpose(1, 2, 0)
    cross = tm_sum(cross, times_all)

    member_all = (group_ids[None, :] == jnp.arange(G, dtype=jnp.int32)[:, None]).astype(jnp.float32)
    counts = jnp.sum(member_all, axis=1)
    pair_count = jnp.maximum(counts * (counts - 1.0), 1.0)
    norm = jnp.sqrt(pair_count * times_all)
    spectrum = cross.transpose(1, 0, 2)
    return spectrum / norm[None, :, None]


def solution(mesh):
    return jax.shard_map(
        body,
        mesh=mesh,
        in_specs=(P("tm", "chan", None), P("tm", "chan", None), P("chan"), P()),
        out_specs=P(None, None, "chan"),
        check_vma=False,
    )
```

```python
import math

import jax
import jax.numpy as jnp
from jax import lax
from jax.sharding import PartitionSpec as P

G = 16
CHAN_PARTS = (("cz", 8), ("cy", 8), ("cc", 2))


def tables(length, minor):
    major = length // minor
    d = jnp.arange(length, dtype=jnp.int32)
    c1 = jnp.arange(major, dtype=jnp.int32)
    c0 = jnp.arange(minor, dtype=jnp.int32)
    step = 2.0 * math.pi / length
    ka = (d[:, None] * (minor * c1)[None, :]) % length
    kb = (d[:, None] * c0[None, :]) % length
    pa = ka.astype(jnp.float32) * step
    pb = kb.astype(jnp.float32) * step
    ca, sa = jnp.cos(pa)[:, :, None], jnp.sin(pa)[:, :, None]
    cb, sb = jnp.cos(pb)[:, None, :], jnp.sin(pb)[:, None, :]
    scale = 1.0 / math.sqrt(length)
    cos_tab = ((ca * cb - sa * sb) * scale).astype(jnp.bfloat16).reshape(length, length)
    sin_tab = ((sa * cb + ca * sb) * scale).astype(jnp.bfloat16).reshape(length, length)
    return cos_tab, sin_tab


def tm_sum(x, n):
    if n & (n - 1):
        return lax.psum(x, "tm")
    step = 1
    while step < n:
        pairs = [(i, i ^ step) for i in range(n)]
        x = x + lax.ppermute(x, "tm", pairs)
        step *= 2
    return x


def chan_all_to_all(x, parts):
    sizes = [n for _, n in parts]
    rest = x.shape[1:]
    x = x.reshape(*sizes, *rest)
    for k in reversed(range(len(parts))):
        x = lax.all_to_all(x, parts[k][0], k, k, tiled=True)
    return x.reshape(-1, *rest)


def chan_index(parts):
    me = 0
    for name, n in parts:
        me = me * n + lax.axis_index(name)
    return me


def split_dot(a, b):
    hi = lax.reduce_precision(a, exponent_bits=8, mantissa_bits=7)
    lo = a - hi
    b16 = b.astype(jnp.bfloat16)
    return (jnp.dot(hi.astype(jnp.bfloat16), b16, preferred_element_type=jnp.float32)
            + jnp.dot(lo.astype(jnp.bfloat16), b16, preferred_element_type=jnp.float32))


def body(visibilities, flags, taper, group_ids, parts=CHAN_PARTS):
    _, local_chans, column_entries = visibilities.shape
    baselines = column_entries // 8
    n_chan = math.prod(n for _, n in parts)
    channels = local_chans * n_chan
    shard_bl = baselines // n_chan
    shard_cols = shard_bl * 8
    times_all = lax.axis_size("tm")

    keep = (1 - flags[0]).astype(jnp.bfloat16).reshape(local_chans, n_chan, shard_bl)
    spread = (jnp.arange(shard_cols, dtype=jnp.int32)[None, :] // 8
              == jnp.arange(shard_bl, dtype=jnp.int32)[:, None]).astype(jnp.bfloat16)
    keep_cols = jnp.einsum("cjb,bl->jcl", keep, spread, preferred_element_type=jnp.float32)
    shaped = visibilities[0].reshape(local_chans, n_chan, shard_cols).transpose(1, 0, 2)
    tapered = (shaped.astype(jnp.float32) * (keep_cols * taper[None, :, None])).astype(jnp.bfloat16)

    member_full = (group_ids[:, None] == jnp.arange(G, dtype=jnp.int32)[None, :]).astype(jnp.bfloat16)
    member_full = member_full.reshape(n_chan, shard_bl, G)
    sums = jnp.einsum("jcbk,jbg->cgk", tapered.reshape(n_chan, local_chans, shard_bl, 8), member_full,
                      preferred_element_type=jnp.float32)
    sums = sums.reshape(local_chans, G * 8).T
    sums_hi = lax.reduce_precision(sums, exponent_bits=8, mantissa_bits=7)
    sums_lo = sums - sums_hi
    block = local_chans * shard_cols
    pad = -(block + 2 * local_chans) % 128
    payload = jnp.concatenate([
        tapered.reshape(n_chan, block),
        sums_hi.astype(jnp.bfloat16),
        sums_lo.astype(jnp.bfloat16),
        jnp.zeros((n_chan, pad), jnp.bfloat16),
    ], axis=1)
    got = chan_all_to_all(payload.reshape(n_chan, 1, -1), parts).reshape(n_chan, -1)
    turned = got[:, :block].reshape(channels, shard_cols)
    col_parts = got[:, block:block + 2 * local_chans].reshape(n_chan, 2, local_chans)
    col_parts = col_parts.transpose(0, 2, 1).reshape(channels, 2)

    cols = jnp.arange(shard_cols, dtype=jnp.int32)
    target = (cols % 2) * (shard_cols // 2) + cols // 2
    permute = (target[:, None] == cols[None, :]).astype(jnp.bfloat16)
    turned = jnp.dot(turned, permute, preferred_element_type=jnp.float32).astype(jnp.bfloat16)
    extra = 128 - col_parts.shape[1]
    rhs = jnp.concatenate([turned, col_parts, jnp.zeros((channels, extra), jnp.bfloat16)], axis=1)
    cos_tab, sin_tab = tables(channels, 128)
    cos_all = jnp.dot(cos_tab, rhs, preferred_element_type=jnp.float32)
    sin_all = jnp.dot(sin_tab, rhs, preferred_element_type=jnp.float32)
    cos_part, sin_part = cos_all[:, :shard_cols], sin_all[:, :shard_cols]
    col_cos = cos_all[:, shard_cols] + cos_all[:, shard_cols + 1]
    col_sin = sin_all[:, shard_cols] + sin_all[:, shard_cols + 1]

    me = chan_index(parts)
    shard_groups = lax.dynamic_slice_in_dim(group_ids, me * shard_bl, shard_bl)
    member = (shard_groups[:, None] == jnp.arange(G, dtype=jnp.int32)[None, :]).astype(jnp.float32)
    eye_s = jnp.eye(4, dtype=jnp.float32)
    m_pow = (member[:, None, :, None] * eye_s[None, :, None, :]).reshape(shard_bl * 4, G * 4)
    half = shard_cols // 2
    real_part = cos_part[:, :half] + sin_part[:, half:]
    imag_part = cos_part[:, half:] - sin_part[:, :half]
    auto = split_dot(real_part * real_part + imag_part * imag_part, m_pow)

    own_d = channels // n_chan
    payload = jnp.concatenate([
        auto.reshape(n_chan, own_d * G * 4),
        col_cos.reshape(n_chan, own_d),
        col_sin.reshape(n_chan, own_d),
    ], axis=1)
    got = chan_all_to_all(payload, parts)
    auto_own = jnp.sum(got[:, :own_d * G * 4], axis=0).reshape(own_d, G, 4)
    cs = got[:, own_d * G * 4:].reshape(G, 4, 2, 2, own_d)
    group_real = cs[:, :, 0, 0] + cs[:, :, 1, 1]
    group_imag = cs[:, :, 1, 0] - cs[:, :, 0, 1]
    cross = group_real * group_real + group_imag * group_imag - auto_own.transpose(1, 2, 0)
    cross = tm_sum(cross, times_all)

    member_all = (group_ids[None, :] == jnp.arange(G, dtype=jnp.int32)[:, None]).astype(jnp.float32)
    counts = jnp.sum(member_all, axis=1)
    pair_count = jnp.maximum(counts * (counts - 1.0), 1.0)
    norm = jnp.sqrt(pair_count * times_all)
    spectrum = cross.transpose(1, 0, 2)
    return spectrum / norm[None, :, None]


def solution(mesh):
    names = tuple(name for name, _ in CHAN_PARTS)
    split = jax.sharding.Mesh(
        mesh.devices.reshape(*(n for _, n in CHAN_PARTS), mesh.shape["tm"]), names + ("tm",))
    return jax.shard_map(
        body,
        mesh=split,
        in_specs=(P("tm", names, None), P("tm", names, None), P(names), P()),
        out_specs=P(None, None, names),
        check_vma=False,
    )
```

```python
import math

import jax
import jax.numpy as jnp
from jax import lax
from jax.sharding import PartitionSpec as P

G = 16


def tables(length, minor):
    major = length // minor
    d = jnp.arange(length, dtype=jnp.int32)
    c1 = jnp.arange(major, dtype=jnp.int32)
    c0 = jnp.arange(minor, dtype=jnp.int32)
    step = 2.0 * math.pi / length
    ka = (d[:, None] * (minor * c1)[None, :]) % length
    kb = (d[:, None] * c0[None, :]) % length
    pa = ka.astype(jnp.float32) * step
    pb = kb.astype(jnp.float32) * step
    ca, sa = jnp.cos(pa)[:, :, None], jnp.sin(pa)[:, :, None]
    cb, sb = jnp.cos(pb)[:, None, :], jnp.sin(pb)[:, None, :]
    scale = 1.0 / math.sqrt(length)
    cos_tab = ((ca * cb - sa * sb) * scale).astype(jnp.bfloat16).reshape(length, length)
    sin_tab = ((sa * cb + ca * sb) * scale).astype(jnp.bfloat16).reshape(length, length)
    return cos_tab, sin_tab


def tm_sum(x, n):
    if n & (n - 1):
        return lax.psum(x, "tm")
    step = 1
    while step < n:
        width = 2 * step
        pairs = [(i, (i // width) * width + width - 1 - i % width) for i in range(n)]
        x = x + lax.ppermute(x, "tm", pairs)
        step *= 2
    return x


def split_dot(a, b):
    hi = lax.reduce_precision(a, exponent_bits=8, mantissa_bits=7)
    lo = a - hi
    b16 = b.astype(jnp.bfloat16)
    return (jnp.dot(hi.astype(jnp.bfloat16), b16, preferred_element_type=jnp.float32)
            + jnp.dot(lo.astype(jnp.bfloat16), b16, preferred_element_type=jnp.float32))


def body(visibilities, flags, taper, group_ids):
    _, local_chans, column_entries = visibilities.shape
    baselines = column_entries // 8
    n_chan = lax.axis_size("chan")
    channels = local_chans * n_chan
    shard_bl = baselines // n_chan
    shard_cols = shard_bl * 8
    times_all = lax.axis_size("tm")

    keep = (1 - flags[0]).astype(jnp.bfloat16).reshape(local_chans, n_chan, shard_bl)
    spread = (jnp.arange(shard_cols, dtype=jnp.int32)[None, :] // 8
              == jnp.arange(shard_bl, dtype=jnp.int32)[:, None]).astype(jnp.bfloat16)
    keep_cols = jnp.einsum("cjb,bl->jcl", keep, spread, preferred_element_type=jnp.float32)
    shaped = visibilities[0].reshape(local_chans, n_chan, shard_cols).transpose(1, 0, 2)
    tapered = (shaped.astype(jnp.float32) * (keep_cols * taper[None, :, None])).astype(jnp.bfloat16)

    member_full = (group_ids[:, None] == jnp.arange(G, dtype=jnp.int32)[None, :]).astype(jnp.bfloat16)
    member_full = member_full.reshape(n_chan, shard_bl, G)
    sums = jnp.einsum("jcbk,jbg->cgk", tapered.reshape(n_chan, local_chans, shard_bl, 8), member_full,
                      preferred_element_type=jnp.float32)
    sums = sums.reshape(local_chans, G * 8).T
    sums_hi = lax.reduce_precision(sums, exponent_bits=8, mantissa_bits=7)
    sums_lo = sums - sums_hi
    block = local_chans * shard_cols
    pad = -(block + 2 * local_chans) % 128
    payload = jnp.concatenate([
        tapered.reshape(n_chan, block),
        sums_hi.astype(jnp.bfloat16),
        sums_lo.astype(jnp.bfloat16),
        jnp.zeros((n_chan, pad), jnp.bfloat16),
    ], axis=1)
    got = lax.all_to_all(payload.reshape(n_chan, 1, -1), "chan", 0, 0, tiled=True).reshape(n_chan, -1)
    turned = got[:, :block].reshape(channels, shard_cols)
    col_parts = got[:, block:block + 2 * local_chans].reshape(n_chan, 2, local_chans)
    col_parts = col_parts.transpose(0, 2, 1).reshape(channels, 2)

    cols = jnp.arange(shard_cols, dtype=jnp.int32)
    target = (cols % 2) * (shard_cols // 2) + cols // 2
    permute = (target[:, None] == cols[None, :]).astype(jnp.bfloat16)
    turned = jnp.dot(turned, permute, preferred_element_type=jnp.float32).astype(jnp.bfloat16)
    extra = 128 - col_parts.shape[1]
    rhs = jnp.concatenate([turned, col_parts, jnp.zeros((channels, extra), jnp.bfloat16)], axis=1)
    cos_tab, sin_tab = tables(channels, 128)
    cos_all = jnp.dot(cos_tab, rhs, preferred_element_type=jnp.float32)
    sin_all = jnp.dot(sin_tab, rhs, preferred_element_type=jnp.float32)
    cos_part, sin_part = cos_all[:, :shard_cols], sin_all[:, :shard_cols]
    col_cos = cos_all[:, shard_cols] + cos_all[:, shard_cols + 1]
    col_sin = sin_all[:, shard_cols] + sin_all[:, shard_cols + 1]

    me = lax.axis_index("chan")
    shard_groups = lax.dynamic_slice_in_dim(group_ids, me * shard_bl, shard_bl)
    member = (shard_groups[:, None] == jnp.arange(G, dtype=jnp.int32)[None, :]).astype(jnp.float32)
    eye_s = jnp.eye(4, dtype=jnp.float32)
    m_pow = (member[:, None, :, None] * eye_s[None, :, None, :]).reshape(shard_bl * 4, G * 4)
    half = shard_cols // 2
    real_part = cos_part[:, :half] + sin_part[:, half:]
    imag_part = cos_part[:, half:] - sin_part[:, :half]
    auto = split_dot(real_part * real_part + imag_part * imag_part, m_pow)

    own_d = channels // n_chan
    payload = jnp.concatenate([
        auto.reshape(n_chan, own_d * G * 4),
        col_cos.reshape(n_chan, own_d),
        col_sin.reshape(n_chan, own_d),
    ], axis=1)
    got = lax.all_to_all(payload, "chan", 0, 0, tiled=True)
    auto_own = jnp.sum(got[:, :own_d * G * 4], axis=0).reshape(own_d, G, 4)
    cs = got[:, own_d * G * 4:].reshape(G, 4, 2, 2, own_d)
    group_real = cs[:, :, 0, 0] + cs[:, :, 1, 1]
    group_imag = cs[:, :, 1, 0] - cs[:, :, 0, 1]
    cross = group_real * group_real + group_imag * group_imag - auto_own.transpose(1, 2, 0)
    cross = tm_sum(cross, times_all)

    member_all = (group_ids[None, :] == jnp.arange(G, dtype=jnp.int32)[:, None]).astype(jnp.float32)
    counts = jnp.sum(member_all, axis=1)
    pair_count = jnp.maximum(counts * (counts - 1.0), 1.0)
    norm = jnp.sqrt(pair_count * times_all)
    spectrum = cross.transpose(1, 0, 2)
    return spectrum / norm[None, :, None]


def solution(mesh):
    return jax.shard_map(
        body,
        mesh=mesh,
        in_specs=(P("tm", "chan", None), P("tm", "chan", None), P("chan"), P()),
        out_specs=P(None, None, "chan"),
        check_vma=False,
    )
```

```python
import math

import jax
import jax.numpy as jnp
from jax import lax
from jax.sharding import PartitionSpec as P

G = 16


def tables(length, minor):
    major = length // minor
    d = jnp.arange(length, dtype=jnp.int32)
    c1 = jnp.arange(major, dtype=jnp.int32)
    c0 = jnp.arange(minor, dtype=jnp.int32)
    step = 2.0 * math.pi / length
    ka = (d[:, None] * (minor * c1)[None, :]) % length
    kb = (d[:, None] * c0[None, :]) % length
    pa = ka.astype(jnp.float32) * step
    pb = kb.astype(jnp.float32) * step
    ca, sa = jnp.cos(pa)[:, :, None], jnp.sin(pa)[:, :, None]
    cb, sb = jnp.cos(pb)[:, None, :], jnp.sin(pb)[:, None, :]
    scale = 1.0 / math.sqrt(length)
    cos_tab = ((ca * cb - sa * sb) * scale).astype(jnp.bfloat16).reshape(length, length)
    sin_tab = ((sa * cb + ca * sb) * scale).astype(jnp.bfloat16).reshape(length, length)
    return cos_tab, sin_tab


def tm_sum(x, n):
    if n & (n - 1):
        return lax.psum(x, "tm")
    step = 1
    while step < n:
        width = 2 * step
        pairs = [(i, (i // width) * width + width - 1 - i % width) for i in range(n)]
        x = x + lax.ppermute(x, "tm", pairs)
        step *= 2
    return x


def split_dot(a, b):
    hi = lax.reduce_precision(a, exponent_bits=8, mantissa_bits=7)
    lo = a - hi
    b16 = b.astype(jnp.bfloat16)
    return (jnp.dot(hi.astype(jnp.bfloat16), b16, preferred_element_type=jnp.float32)
            + jnp.dot(lo.astype(jnp.bfloat16), b16, preferred_element_type=jnp.float32))


def body(visibilities, flags, taper, group_ids):
    _, local_chans, column_entries = visibilities.shape
    baselines = column_entries // 8
    n_chan = lax.axis_size("chan")
    channels = local_chans * n_chan
    shard_bl = baselines // n_chan
    shard_cols = shard_bl * 8
    times_all = lax.axis_size("tm")

    keep = (1 - flags[0]).astype(jnp.bfloat16).reshape(local_chans, n_chan, shard_bl)
    spread = (jnp.arange(shard_cols, dtype=jnp.int32)[None, :] // 8
              == jnp.arange(shard_bl, dtype=jnp.int32)[:, None]).astype(jnp.bfloat16)
    keep_cols = jnp.einsum("cjb,bl->jcl", keep, spread, preferred_element_type=jnp.float32)
    shaped = visibilities[0].reshape(local_chans, n_chan, shard_cols).transpose(1, 0, 2)
    tapered = (shaped.astype(jnp.float32) * (keep_cols * taper[None, :, None])).astype(jnp.bfloat16)

    member_full = (group_ids[:, None] == jnp.arange(G, dtype=jnp.int32)[None, :]).astype(jnp.bfloat16)
    member_full = member_full.reshape(n_chan, shard_bl, G)
    sums = jnp.einsum("jcbk,jbg->cgk", tapered.reshape(n_chan, local_chans, shard_bl, 8), member_full,
                      preferred_element_type=jnp.float32)
    sums = sums.reshape(local_chans, G * 8).T
    sums_hi = lax.reduce_precision(sums, exponent_bits=8, mantissa_bits=7)
    sums_lo = sums - sums_hi
    pad = shard_cols - 2 * local_chans
    extra_row = jnp.concatenate([
        sums_hi.astype(jnp.bfloat16),
        sums_lo.astype(jnp.bfloat16),
        jnp.zeros((n_chan, pad), jnp.bfloat16),
    ], axis=1)
    payload = jnp.concatenate([tapered, extra_row[:, None, :]], axis=1)
    got = lax.all_to_all(payload, "chan", 0, 0, tiled=True)
    turned = got[:, :local_chans, :].reshape(channels, shard_cols)
    col_parts = got[:, local_chans, :2 * local_chans].reshape(n_chan, 2, local_chans)
    col_parts = col_parts.transpose(0, 2, 1).reshape(channels, 2)

    cols = jnp.arange(shard_cols, dtype=jnp.int32)
    target = (cols % 2) * (shard_cols // 2) + cols // 2
    permute = (target[:, None] == cols[None, :]).astype(jnp.bfloat16)
    turned = jnp.dot(turned, permute, preferred_element_type=jnp.float32).astype(jnp.bfloat16)
    extra = 128 - col_parts.shape[1]
    rhs = jnp.concatenate([turned, col_parts, jnp.zeros((channels, extra), jnp.bfloat16)], axis=1)
    cos_tab, sin_tab = tables(channels, 128)
    cos_all = jnp.dot(cos_tab, rhs, preferred_element_type=jnp.float32)
    sin_all = jnp.dot(sin_tab, rhs, preferred_element_type=jnp.float32)
    cos_part, sin_part = cos_all[:, :shard_cols], sin_all[:, :shard_cols]
    col_cos = cos_all[:, shard_cols] + cos_all[:, shard_cols + 1]
    col_sin = sin_all[:, shard_cols] + sin_all[:, shard_cols + 1]

    me = lax.axis_index("chan")
    shard_groups = lax.dynamic_slice_in_dim(group_ids, me * shard_bl, shard_bl)
    member = (shard_groups[:, None] == jnp.arange(G, dtype=jnp.int32)[None, :]).astype(jnp.float32)
    eye_s = jnp.eye(4, dtype=jnp.float32)
    m_pow = (member[:, None, :, None] * eye_s[None, :, None, :]).reshape(shard_bl * 4, G * 4)
    half = shard_cols // 2
    real_part = cos_part[:, :half] + sin_part[:, half:]
    imag_part = cos_part[:, half:] - sin_part[:, :half]
    auto = split_dot(real_part * real_part + imag_part * imag_part, m_pow)

    own_d = channels // n_chan
    payload = jnp.concatenate([
        auto.reshape(n_chan, own_d * G * 4),
        col_cos.reshape(n_chan, own_d),
        col_sin.reshape(n_chan, own_d),
    ], axis=1)
    got = lax.all_to_all(payload, "chan", 0, 0, tiled=True)
    auto_own = jnp.sum(got[:, :own_d * G * 4], axis=0).reshape(own_d, G, 4)
    cs = got[:, own_d * G * 4:].reshape(G, 4, 2, 2, own_d)
    group_real = cs[:, :, 0, 0] + cs[:, :, 1, 1]
    group_imag = cs[:, :, 1, 0] - cs[:, :, 0, 1]
    cross = group_real * group_real + group_imag * group_imag - auto_own.transpose(1, 2, 0)
    cross = tm_sum(cross, times_all)

    member_all = (group_ids[None, :] == jnp.arange(G, dtype=jnp.int32)[:, None]).astype(jnp.float32)
    counts = jnp.sum(member_all, axis=1)
    pair_count = jnp.maximum(counts * (counts - 1.0), 1.0)
    norm = jnp.sqrt(pair_count * times_all)
    spectrum = cross.transpose(1, 0, 2)
    return spectrum / norm[None, :, None]


def solution(mesh):
    return jax.shard_map(
        body,
        mesh=mesh,
        in_specs=(P("tm", "chan", None), P("tm", "chan", None), P("chan"), P()),
        out_specs=P(None, None, "chan"),
        check_vma=False,
    )
```

```python
import math

import jax
import jax.numpy as jnp
from jax import lax
from jax.sharding import PartitionSpec as P

G = 16


def tables(length, minor):
    major = length // minor
    d = jnp.arange(length, dtype=jnp.int32)
    c1 = jnp.arange(major, dtype=jnp.int32)
    c0 = jnp.arange(minor, dtype=jnp.int32)
    step = 2.0 * math.pi / length
    ka = (d[:, None] * (minor * c1)[None, :]) % length
    kb = (d[:, None] * c0[None, :]) % length
    pa = ka.astype(jnp.float32) * step
    pb = kb.astype(jnp.float32) * step
    ca, sa = jnp.cos(pa)[:, :, None], jnp.sin(pa)[:, :, None]
    cb, sb = jnp.cos(pb)[:, None, :], jnp.sin(pb)[:, None, :]
    scale = 1.0 / math.sqrt(length)
    cos_tab = ((ca * cb - sa * sb) * scale).astype(jnp.bfloat16).reshape(length, length)
    sin_tab = ((sa * cb + ca * sb) * scale).astype(jnp.bfloat16).reshape(length, length)
    return cos_tab, sin_tab


def tm_sum(x, n):
    got = lax.all_to_all(jnp.broadcast_to(x[None], (n, *x.shape)), "tm", 0, 0, tiled=True)
    while got.shape[0] > 1:
        if got.shape[0] % 2:
            got = jnp.concatenate([got[:1] + got[1:2], got[2:]])
        else:
            got = got[0::2] + got[1::2]
    return got[0]


def split_dot(a, b):
    hi = lax.reduce_precision(a, exponent_bits=8, mantissa_bits=7)
    lo = a - hi
    b16 = b.astype(jnp.bfloat16)
    return (jnp.dot(hi.astype(jnp.bfloat16), b16, preferred_element_type=jnp.float32)
            + jnp.dot(lo.astype(jnp.bfloat16), b16, preferred_element_type=jnp.float32))


def body(visibilities, flags, taper, group_ids):
    _, local_chans, column_entries = visibilities.shape
    baselines = column_entries // 8
    n_chan = lax.axis_size("chan")
    channels = local_chans * n_chan
    shard_bl = baselines // n_chan
    shard_cols = shard_bl * 8
    times_all = lax.axis_size("tm")

    keep = (1 - flags[0]).astype(jnp.bfloat16).reshape(local_chans, n_chan, shard_bl)
    spread = (jnp.arange(shard_cols, dtype=jnp.int32)[None, :] // 8
              == jnp.arange(shard_bl, dtype=jnp.int32)[:, None]).astype(jnp.bfloat16)
    keep_cols = jnp.einsum("cjb,bl->jcl", keep, spread, preferred_element_type=jnp.float32)
    shaped = visibilities[0].reshape(local_chans, n_chan, shard_cols).transpose(1, 0, 2)
    tapered = (shaped.astype(jnp.float32) * (keep_cols * taper[None, :, None])).astype(jnp.bfloat16)

    member_full = (group_ids[:, None] == jnp.arange(G, dtype=jnp.int32)[None, :]).astype(jnp.bfloat16)
    member_full = member_full.reshape(n_chan, shard_bl, G)
    sums = jnp.einsum("jcbk,jbg->cgk", tapered.reshape(n_chan, local_chans, shard_bl, 8), member_full,
                      preferred_element_type=jnp.float32)
    sums = sums.reshape(local_chans, G * 8).T
    sums_hi = lax.reduce_precision(sums, exponent_bits=8, mantissa_bits=7)
    sums_lo = sums - sums_hi
    pad = shard_cols - 2 * local_chans
    extra_row = jnp.concatenate([
        sums_hi.astype(jnp.bfloat16),
        sums_lo.astype(jnp.bfloat16),
        jnp.zeros((n_chan, pad), jnp.bfloat16),
    ], axis=1)
    payload = jnp.concatenate([tapered, extra_row[:, None, :]], axis=1)
    got = lax.all_to_all(payload, "chan", 0, 0, tiled=True)
    turned = got[:, :local_chans, :].reshape(channels, shard_cols)
    col_parts = got[:, local_chans, :2 * local_chans].reshape(n_chan, 2, local_chans)
    col_parts = col_parts.transpose(0, 2, 1).reshape(channels, 2)

    cols = jnp.arange(shard_cols, dtype=jnp.int32)
    target = (cols % 2) * (shard_cols // 2) + cols // 2
    permute = (target[:, None] == cols[None, :]).astype(jnp.bfloat16)
    turned = jnp.dot(turned, permute, preferred_element_type=jnp.float32).astype(jnp.bfloat16)
    extra = 128 - col_parts.shape[1]
    rhs = jnp.concatenate([turned, col_parts, jnp.zeros((channels, extra), jnp.bfloat16)], axis=1)
    cos_tab, sin_tab = tables(channels, 128)
    cos_all = jnp.dot(cos_tab, rhs, preferred_element_type=jnp.float32)
    sin_all = jnp.dot(sin_tab, rhs, preferred_element_type=jnp.float32)
    cos_part, sin_part = cos_all[:, :shard_cols], sin_all[:, :shard_cols]
    col_cos = cos_all[:, shard_cols] + cos_all[:, shard_cols + 1]
    col_sin = sin_all[:, shard_cols] + sin_all[:, shard_cols + 1]

    me = lax.axis_index("chan")
    shard_groups = lax.dynamic_slice_in_dim(group_ids, me * shard_bl, shard_bl)
    member = (shard_groups[:, None] == jnp.arange(G, dtype=jnp.int32)[None, :]).astype(jnp.float32)
    eye_s = jnp.eye(4, dtype=jnp.float32)
    m_pow = (member[:, None, :, None] * eye_s[None, :, None, :]).reshape(shard_bl * 4, G * 4)
    half = shard_cols // 2
    real_part = cos_part[:, :half] + sin_part[:, half:]
    imag_part = cos_part[:, half:] - sin_part[:, :half]
    auto = split_dot(real_part * real_part + imag_part * imag_part, m_pow)

    own_d = channels // n_chan
    payload = jnp.concatenate([
        auto.reshape(n_chan, own_d * G * 4),
        col_cos.reshape(n_chan, own_d),
        col_sin.reshape(n_chan, own_d),
    ], axis=1)
    got = lax.all_to_all(payload, "chan", 0, 0, tiled=True)
    auto_own = jnp.sum(got[:, :own_d * G * 4], axis=0).reshape(own_d, G, 4)
    cs = got[:, own_d * G * 4:].reshape(G, 4, 2, 2, own_d)
    group_real = cs[:, :, 0, 0] + cs[:, :, 1, 1]
    group_imag = cs[:, :, 1, 0] - cs[:, :, 0, 1]
    cross = group_real * group_real + group_imag * group_imag - auto_own.transpose(1, 2, 0)
    cross = tm_sum(cross, times_all)

    member_all = (group_ids[None, :] == jnp.arange(G, dtype=jnp.int32)[:, None]).astype(jnp.float32)
    counts = jnp.sum(member_all, axis=1)
    pair_count = jnp.maximum(counts * (counts - 1.0), 1.0)
    norm = jnp.sqrt(pair_count * times_all)
    spectrum = cross.transpose(1, 0, 2)
    return spectrum / norm[None, :, None]


def solution(mesh):
    return jax.shard_map(
        body,
        mesh=mesh,
        in_specs=(P("tm", "chan", None), P("tm", "chan", None), P("chan"), P()),
        out_specs=P(None, None, "chan"),
        check_vma=False,
    )
```

```python
import math

import jax
import jax.numpy as jnp
from jax import lax
from jax.sharding import PartitionSpec as P

G = 16


def tables(length, minor):
    major = length // minor
    d = jnp.arange(length, dtype=jnp.int32)
    c1 = jnp.arange(major, dtype=jnp.int32)
    c0 = jnp.arange(minor, dtype=jnp.int32)
    step = 2.0 * math.pi / length
    ka = (d[:, None] * (minor * c1)[None, :]) % length
    kb = (d[:, None] * c0[None, :]) % length
    pa = ka.astype(jnp.float32) * step
    pb = kb.astype(jnp.float32) * step
    ca, sa = jnp.cos(pa)[:, :, None], jnp.sin(pa)[:, :, None]
    cb, sb = jnp.cos(pb)[:, None, :], jnp.sin(pb)[:, None, :]
    scale = 1.0 / math.sqrt(length)
    cos_tab = ((ca * cb - sa * sb) * scale).astype(jnp.bfloat16).reshape(length, length)
    sin_tab = ((sa * cb + ca * sb) * scale).astype(jnp.bfloat16).reshape(length, length)
    return cos_tab, sin_tab


def tm_sum(x, n):
    flat = jnp.broadcast_to(x.reshape(1, 1, -1), (n, 1, x.size))
    got = lax.all_to_all(flat, "tm", 0, 0, tiled=True)[:, 0]
    while got.shape[0] > 1:
        if got.shape[0] % 2:
            got = jnp.concatenate([got[:1] + got[1:2], got[2:]])
        else:
            got = got[0::2] + got[1::2]
    return got[0].reshape(x.shape)


def split_dot(a, b):
    hi = lax.reduce_precision(a, exponent_bits=8, mantissa_bits=7)
    lo = a - hi
    b16 = b.astype(jnp.bfloat16)
    return (jnp.dot(hi.astype(jnp.bfloat16), b16, preferred_element_type=jnp.float32)
            + jnp.dot(lo.astype(jnp.bfloat16), b16, preferred_element_type=jnp.float32))


def body(visibilities, flags, taper, group_ids):
    _, local_chans, column_entries = visibilities.shape
    baselines = column_entries // 8
    n_chan = lax.axis_size("chan")
    channels = local_chans * n_chan
    shard_bl = baselines // n_chan
    shard_cols = shard_bl * 8
    times_all = lax.axis_size("tm")

    keep = (1 - flags[0]).astype(jnp.bfloat16).reshape(local_chans, n_chan, shard_bl)
    spread = (jnp.arange(shard_cols, dtype=jnp.int32)[None, :] // 8
              == jnp.arange(shard_bl, dtype=jnp.int32)[:, None]).astype(jnp.bfloat16)
    keep_cols = jnp.einsum("cjb,bl->jcl", keep, spread, preferred_element_type=jnp.float32)
    shaped = visibilities[0].reshape(local_chans, n_chan, shard_cols).transpose(1, 0, 2)
    tapered = (shaped.astype(jnp.float32) * (keep_cols * taper[None, :, None])).astype(jnp.bfloat16)

    member_full = (group_ids[:, None] == jnp.arange(G, dtype=jnp.int32)[None, :]).astype(jnp.bfloat16)
    member_full = member_full.reshape(n_chan, shard_bl, G)
    sums = jnp.einsum("jcbk,jbg->cgk", tapered.reshape(n_chan, local_chans, shard_bl, 8), member_full,
                      preferred_element_type=jnp.float32)
    sums = sums.reshape(local_chans, G * 8).T
    sums_hi = lax.reduce_precision(sums, exponent_bits=8, mantissa_bits=7)
    sums_lo = sums - sums_hi
    pad = shard_cols - 2 * local_chans
    extra_row = jnp.concatenate([
        sums_hi.astype(jnp.bfloat16),
        sums_lo.astype(jnp.bfloat16),
        jnp.zeros((n_chan, pad), jnp.bfloat16),
    ], axis=1)
    payload = jnp.concatenate([tapered, extra_row[:, None, :]], axis=1)
    got = lax.all_to_all(payload, "chan", 0, 0, tiled=True)
    turned = got[:, :local_chans, :].reshape(channels, shard_cols)
    col_parts = got[:, local_chans, :2 * local_chans].reshape(n_chan, 2, local_chans)
    col_parts = col_parts.transpose(0, 2, 1).reshape(channels, 2)

    cols = jnp.arange(shard_cols, dtype=jnp.int32)
    target = (cols % 2) * (shard_cols // 2) + cols // 2
    permute = (target[:, None] == cols[None, :]).astype(jnp.bfloat16)
    turned = jnp.dot(turned, permute, preferred_element_type=jnp.float32).astype(jnp.bfloat16)
    extra = 128 - col_parts.shape[1]
    rhs = jnp.concatenate([turned, col_parts, jnp.zeros((channels, extra), jnp.bfloat16)], axis=1)
    cos_tab, sin_tab = tables(channels, 128)
    cos_all = jnp.dot(cos_tab, rhs, preferred_element_type=jnp.float32)
    sin_all = jnp.dot(sin_tab, rhs, preferred_element_type=jnp.float32)
    cos_part, sin_part = cos_all[:, :shard_cols], sin_all[:, :shard_cols]
    col_cos = cos_all[:, shard_cols] + cos_all[:, shard_cols + 1]
    col_sin = sin_all[:, shard_cols] + sin_all[:, shard_cols + 1]

    me = lax.axis_index("chan")
    shard_groups = lax.dynamic_slice_in_dim(group_ids, me * shard_bl, shard_bl)
    member = (shard_groups[:, None] == jnp.arange(G, dtype=jnp.int32)[None, :]).astype(jnp.float32)
    eye_s = jnp.eye(4, dtype=jnp.float32)
    m_pow = (member[:, None, :, None] * eye_s[None, :, None, :]).reshape(shard_bl * 4, G * 4)
    half = shard_cols // 2
    real_part = cos_part[:, :half] + sin_part[:, half:]
    imag_part = cos_part[:, half:] - sin_part[:, :half]
    auto = split_dot(real_part * real_part + imag_part * imag_part, m_pow)

    own_d = channels // n_chan
    payload = jnp.concatenate([
        auto.reshape(n_chan, own_d * G * 4),
        col_cos.reshape(n_chan, own_d),
        col_sin.reshape(n_chan, own_d),
    ], axis=1)
    got = lax.all_to_all(payload, "chan", 0, 0, tiled=True)
    auto_own = jnp.sum(got[:, :own_d * G * 4], axis=0).reshape(own_d, G, 4)
    cs = got[:, own_d * G * 4:].reshape(G, 4, 2, 2, own_d)
    cs = cs.transpose(1, 0, 2, 3, 4)
    group_real = cs[:, :, 0, 0] + cs[:, :, 1, 1]
    group_imag = cs[:, :, 1, 0] - cs[:, :, 0, 1]
    cross = group_real * group_real + group_imag * group_imag - auto_own.transpose(2, 1, 0)
    cross = tm_sum(cross, times_all)

    member_all = (group_ids[None, :] == jnp.arange(G, dtype=jnp.int32)[:, None]).astype(jnp.float32)
    counts = jnp.sum(member_all, axis=1)
    pair_count = jnp.maximum(counts * (counts - 1.0), 1.0)
    norm = jnp.sqrt(pair_count * times_all)
    return cross / norm[None, :, None]


def solution(mesh):
    return jax.shard_map(
        body,
        mesh=mesh,
        in_specs=(P("tm", "chan", None), P("tm", "chan", None), P("chan"), P()),
        out_specs=P(None, None, "chan"),
        check_vma=False,
    )
```

```python
import math

import jax
import jax.numpy as jnp
from jax import lax
from jax.sharding import PartitionSpec as P

G = 16


def tables(length, minor):
    major = length // minor
    d = jnp.arange(length, dtype=jnp.int32)
    c1 = jnp.arange(major, dtype=jnp.int32)
    c0 = jnp.arange(minor, dtype=jnp.int32)
    step = 2.0 * math.pi / length
    ka = (d[:, None] * (minor * c1)[None, :]) % length
    kb = (d[:, None] * c0[None, :]) % length
    pa = ka.astype(jnp.float32) * step
    pb = kb.astype(jnp.float32) * step
    ca, sa = jnp.cos(pa)[:, :, None], jnp.sin(pa)[:, :, None]
    cb, sb = jnp.cos(pb)[:, None, :], jnp.sin(pb)[:, None, :]
    scale = 1.0 / math.sqrt(length)
    cos_tab = ((ca * cb - sa * sb) * scale).astype(jnp.bfloat16).reshape(length, length)
    sin_tab = ((sa * cb + ca * sb) * scale).astype(jnp.bfloat16).reshape(length, length)
    return cos_tab, sin_tab


def tm_sum(x, n):
    flat = jnp.broadcast_to(x.reshape(1, 1, -1), (n, 1, x.size))
    got = lax.all_to_all(flat, "tm", 0, 0, tiled=True)[:, 0]
    while got.shape[0] > 1:
        if got.shape[0] % 2:
            got = jnp.concatenate([got[:1] + got[1:2], got[2:]])
        else:
            got = got[0::2] + got[1::2]
    return got[0].reshape(x.shape)


def split_dot(a, b):
    hi = lax.reduce_precision(a, exponent_bits=8, mantissa_bits=7)
    lo = a - hi
    b16 = b.astype(jnp.bfloat16)
    return (jnp.dot(hi.astype(jnp.bfloat16), b16, preferred_element_type=jnp.float32)
            + jnp.dot(lo.astype(jnp.bfloat16), b16, preferred_element_type=jnp.float32))


def body(visibilities, flags, taper, group_ids):
    _, local_chans, column_entries = visibilities.shape
    baselines = column_entries // 8
    n_chan = lax.axis_size("chan")
    channels = local_chans * n_chan
    shard_bl = baselines // n_chan
    shard_cols = shard_bl * 8
    times_all = lax.axis_size("tm")

    keep = (1 - flags[0]).astype(jnp.bfloat16).reshape(local_chans, n_chan, shard_bl)
    spread = (jnp.arange(shard_cols, dtype=jnp.int32)[None, :] // 8
              == jnp.arange(shard_bl, dtype=jnp.int32)[:, None]).astype(jnp.bfloat16)
    keep_cols = jnp.einsum("cjb,bl->jcl", keep, spread, preferred_element_type=jnp.float32)
    shaped = visibilities[0].reshape(local_chans, n_chan, shard_cols).transpose(1, 0, 2)
    tapered = (shaped.astype(jnp.float32) * (keep_cols * taper[None, :, None])).astype(jnp.bfloat16)

    member_full = (group_ids[:, None] == jnp.arange(G, dtype=jnp.int32)[None, :]).astype(jnp.bfloat16)
    member_full = member_full.reshape(n_chan, shard_bl, G)
    sums = jnp.einsum("jcbk,jbg->cgk", tapered.reshape(n_chan, local_chans, shard_bl, 8), member_full,
                      preferred_element_type=jnp.float32)
    sums = sums.reshape(local_chans, G * 8).T
    sums_hi = lax.reduce_precision(sums, exponent_bits=8, mantissa_bits=7)
    sums_lo = sums - sums_hi
    block = local_chans * shard_cols
    pad = -(block + 2 * local_chans) % 128
    payload = jnp.concatenate([
        tapered.reshape(n_chan, block),
        sums_hi.astype(jnp.bfloat16),
        sums_lo.astype(jnp.bfloat16),
        jnp.zeros((n_chan, pad), jnp.bfloat16),
    ], axis=1)
    got = lax.all_to_all(payload.reshape(n_chan, 1, -1), "chan", 0, 0, tiled=True).reshape(n_chan, -1)
    turned = got[:, :block].reshape(channels, shard_cols)
    col_parts = got[:, block:block + 2 * local_chans].reshape(n_chan, 2, local_chans)
    col_parts = col_parts.transpose(0, 2, 1).reshape(channels, 2)

    cols = jnp.arange(shard_cols, dtype=jnp.int32)
    target = (cols % 2) * (shard_cols // 2) + cols // 2
    permute = (target[:, None] == cols[None, :]).astype(jnp.bfloat16)
    turned = jnp.dot(turned, permute, preferred_element_type=jnp.float32).astype(jnp.bfloat16)
    extra = 128 - col_parts.shape[1]
    rhs = jnp.concatenate([turned, col_parts, jnp.zeros((channels, extra), jnp.bfloat16)], axis=1)
    cos_tab, sin_tab = tables(channels, 128)
    cos_all = jnp.dot(cos_tab, rhs, preferred_element_type=jnp.float32)
    sin_all = jnp.dot(sin_tab, rhs, preferred_element_type=jnp.float32)
    cos_part, sin_part = cos_all[:, :shard_cols], sin_all[:, :shard_cols]
    col_cos = cos_all[:, shard_cols] + cos_all[:, shard_cols + 1]
    col_sin = sin_all[:, shard_cols] + sin_all[:, shard_cols + 1]

    me = lax.axis_index("chan")
    shard_groups = lax.dynamic_slice_in_dim(group_ids, me * shard_bl, shard_bl)
    member = (shard_groups[:, None] == jnp.arange(G, dtype=jnp.int32)[None, :]).astype(jnp.float32)
    eye_s = jnp.eye(4, dtype=jnp.float32)
    m_pow = (member[:, None, :, None] * eye_s[None, :, None, :]).reshape(shard_bl * 4, G * 4)
    half = shard_cols // 2
    real_part = cos_part[:, :half] + sin_part[:, half:]
    imag_part = cos_part[:, half:] - sin_part[:, :half]
    auto = split_dot(real_part * real_part + imag_part * imag_part, m_pow)

    own_d = channels // n_chan
    payload = jnp.concatenate([
        auto.reshape(n_chan, own_d * G * 4),
        col_cos.reshape(n_chan, own_d),
        col_sin.reshape(n_chan, own_d),
    ], axis=1)
    got = lax.all_to_all(payload, "chan", 0, 0, tiled=True)
    auto_own = jnp.sum(got[:, :own_d * G * 4], axis=0).reshape(own_d, G, 4)
    cs = got[:, own_d * G * 4:].reshape(G, 4, 2, 2, own_d)
    cs = cs.transpose(1, 0, 2, 3, 4)
    group_real = cs[:, :, 0, 0] + cs[:, :, 1, 1]
    group_imag = cs[:, :, 1, 0] - cs[:, :, 0, 1]
    cross = group_real * group_real + group_imag * group_imag - auto_own.transpose(2, 1, 0)
    cross = tm_sum(cross, times_all)

    member_all = (group_ids[None, :] == jnp.arange(G, dtype=jnp.int32)[:, None]).astype(jnp.float32)
    counts = jnp.sum(member_all, axis=1)
    pair_count = jnp.maximum(counts * (counts - 1.0), 1.0)
    norm = jnp.sqrt(pair_count * times_all)
    return cross / norm[None, :, None]


def solution(mesh):
    return jax.shard_map(
        body,
        mesh=mesh,
        in_specs=(P("tm", "chan", None), P("tm", "chan", None), P("chan"), P()),
        out_specs=P(None, None, "chan"),
        check_vma=False,
    )
```

```python
import math

import jax
import jax.numpy as jnp
from jax import lax
from jax.sharding import PartitionSpec as P

G = 16


def tables(length, minor):
    major = length // minor
    d = jnp.arange(length, dtype=jnp.int32)
    c1 = jnp.arange(major, dtype=jnp.int32)
    c0 = jnp.arange(minor, dtype=jnp.int32)
    step = 2.0 * math.pi / length
    ka = (d[:, None] * (minor * c1)[None, :]) % length
    kb = (d[:, None] * c0[None, :]) % length
    pa = ka.astype(jnp.float32) * step
    pb = kb.astype(jnp.float32) * step
    ca, sa = jnp.cos(pa)[:, :, None], jnp.sin(pa)[:, :, None]
    cb, sb = jnp.cos(pb)[:, None, :], jnp.sin(pb)[:, None, :]
    scale = 1.0 / math.sqrt(length)
    cos_tab = ((ca * cb - sa * sb) * scale).astype(jnp.bfloat16).reshape(length, length)
    sin_tab = ((sa * cb + ca * sb) * scale).astype(jnp.bfloat16).reshape(length, length)
    return cos_tab, sin_tab


def tm_sum(x, n):
    flat = jnp.broadcast_to(x.reshape(1, 1, -1), (n, 1, x.size))
    got = lax.all_to_all(flat, "tm", 0, 0, tiled=True)[:, 0]
    while got.shape[0] > 1:
        if got.shape[0] % 2:
            got = jnp.concatenate([got[:1] + got[1:2], got[2:]])
        else:
            got = got[0::2] + got[1::2]
    return got[0].reshape(x.shape)


def split_dot(a, b):
    hi = lax.reduce_precision(a, exponent_bits=8, mantissa_bits=7)
    lo = a - hi
    b16 = b.astype(jnp.bfloat16)
    return (jnp.dot(hi.astype(jnp.bfloat16), b16, preferred_element_type=jnp.float32)
            + jnp.dot(lo.astype(jnp.bfloat16), b16, preferred_element_type=jnp.float32))


def body(visibilities, flags, taper, group_ids):
    _, local_chans, column_entries = visibilities.shape
    baselines = column_entries // 8
    n_chan = lax.axis_size("chan")
    channels = local_chans * n_chan
    shard_bl = baselines // n_chan
    shard_cols = shard_bl * 8
    times_all = lax.axis_size("tm")

    half = shard_cols // 2
    cols = jnp.arange(shard_cols, dtype=jnp.int32)
    target = (cols % 2) * half + cols // 2
    permute = (target[:, None] == cols[None, :]).astype(jnp.bfloat16)
    keep = (1 - flags[0]).astype(jnp.bfloat16).reshape(local_chans, n_chan, shard_bl)
    spread = ((cols[None, :] % half) // 4
              == jnp.arange(shard_bl, dtype=jnp.int32)[:, None]).astype(jnp.bfloat16)
    keep_cols = jnp.einsum("cjb,bl->jcl", keep, spread, preferred_element_type=jnp.float32)
    shaped = visibilities[0].reshape(local_chans, n_chan, shard_cols).transpose(1, 0, 2)
    shaped = jnp.dot(shaped, permute, preferred_element_type=jnp.float32)
    tapered = (shaped * (keep_cols * taper[None, :, None])).astype(jnp.bfloat16)

    member_full = (group_ids[:, None] == jnp.arange(G, dtype=jnp.int32)[None, :]).astype(jnp.bfloat16)
    member_full = member_full.reshape(n_chan, shard_bl, G)
    sums = jnp.einsum("jcrbs,jbg->cgsr", tapered.reshape(n_chan, local_chans, 2, shard_bl, 4), member_full,
                      preferred_element_type=jnp.float32)
    sums = sums.reshape(local_chans, G * 8).T
    sums_hi = lax.reduce_precision(sums, exponent_bits=8, mantissa_bits=7)
    sums_lo = sums - sums_hi
    pad = shard_cols - 2 * local_chans
    extra_row = jnp.concatenate([
        sums_hi.astype(jnp.bfloat16),
        sums_lo.astype(jnp.bfloat16),
        jnp.zeros((n_chan, pad), jnp.bfloat16),
    ], axis=1)
    payload = jnp.concatenate([tapered, extra_row[:, None, :]], axis=1)
    got = lax.all_to_all(payload, "chan", 0, 0, tiled=True)
    turned = got[:, :local_chans, :].reshape(channels, shard_cols)
    col_parts = got[:, local_chans, :2 * local_chans].reshape(n_chan, 2, local_chans)
    col_parts = col_parts.transpose(0, 2, 1).reshape(channels, 2)

    extra = 128 - col_parts.shape[1]
    rhs = jnp.concatenate([turned, col_parts, jnp.zeros((channels, extra), jnp.bfloat16)], axis=1)
    cos_tab, sin_tab = tables(channels, 128)
    cos_all = jnp.dot(cos_tab, rhs, preferred_element_type=jnp.float32)
    sin_all = jnp.dot(sin_tab, rhs, preferred_element_type=jnp.float32)
    cos_part, sin_part = cos_all[:, :shard_cols], sin_all[:, :shard_cols]
    col_cos = cos_all[:, shard_cols] + cos_all[:, shard_cols + 1]
    col_sin = sin_all[:, shard_cols] + sin_all[:, shard_cols + 1]

    me = lax.axis_index("chan")
    shard_groups = lax.dynamic_slice_in_dim(group_ids, me * shard_bl, shard_bl)
    member = (shard_groups[:, None] == jnp.arange(G, dtype=jnp.int32)[None, :]).astype(jnp.float32)
    eye_s = jnp.eye(4, dtype=jnp.float32)
    m_pow = (member[:, None, :, None] * eye_s[None, :, None, :]).reshape(shard_bl * 4, G * 4)
    real_part = cos_part[:, :half] + sin_part[:, half:]
    imag_part = cos_part[:, half:] - sin_part[:, :half]
    auto = split_dot(real_part * real_part + imag_part * imag_part, m_pow)

    own_d = channels // n_chan
    payload = jnp.concatenate([
        auto.reshape(n_chan, own_d * G * 4),
        col_cos.reshape(n_chan, own_d),
        col_sin.reshape(n_chan, own_d),
    ], axis=1)
    got = lax.all_to_all(payload, "chan", 0, 0, tiled=True)
    auto_own = jnp.sum(got[:, :own_d * G * 4], axis=0).reshape(own_d, G, 4)
    cs = got[:, own_d * G * 4:].reshape(G, 4, 2, 2, own_d)
    cs = cs.transpose(1, 0, 2, 3, 4)
    group_real = cs[:, :, 0, 0] + cs[:, :, 1, 1]
    group_imag = cs[:, :, 1, 0] - cs[:, :, 0, 1]
    cross = group_real * group_real + group_imag * group_imag - auto_own.transpose(2, 1, 0)
    cross = tm_sum(cross, times_all)

    member_all = (group_ids[None, :] == jnp.arange(G, dtype=jnp.int32)[:, None]).astype(jnp.float32)
    counts = jnp.sum(member_all, axis=1)
    pair_count = jnp.maximum(counts * (counts - 1.0), 1.0)
    norm = jnp.sqrt(pair_count * times_all)
    return cross / norm[None, :, None]


def solution(mesh):
    return jax.shard_map(
        body,
        mesh=mesh,
        in_specs=(P("tm", "chan", None), P("tm", "chan", None), P("chan"), P()),
        out_specs=P(None, None, "chan"),
        check_vma=False,
    )
```

```python
import math

import jax
import jax.numpy as jnp
from jax import lax
from jax.sharding import PartitionSpec as P

G = 16


def tables(length, minor):
    major = length // minor
    d = jnp.arange(length, dtype=jnp.int32)
    c1 = jnp.arange(major, dtype=jnp.int32)
    c0 = jnp.arange(minor, dtype=jnp.int32)
    step = 2.0 * math.pi / length
    ka = (d[:, None] * (minor * c1)[None, :]) % length
    kb = (d[:, None] * c0[None, :]) % length
    pa = ka.astype(jnp.float32) * step
    pb = kb.astype(jnp.float32) * step
    ca, sa = jnp.cos(pa)[:, :, None], jnp.sin(pa)[:, :, None]
    cb, sb = jnp.cos(pb)[:, None, :], jnp.sin(pb)[:, None, :]
    scale = 1.0 / math.sqrt(length)
    cos_tab = ((ca * cb - sa * sb) * scale).astype(jnp.bfloat16).reshape(length, length)
    sin_tab = ((sa * cb + ca * sb) * scale).astype(jnp.bfloat16).reshape(length, length)
    return cos_tab, sin_tab


def tm_sum(x, n):
    flat = jnp.broadcast_to(x.reshape(1, 1, -1), (n, 1, x.size))
    got = lax.all_to_all(flat, "tm", 0, 0, tiled=True)[:, 0]
    while got.shape[0] > 1:
        if got.shape[0] % 2:
            got = jnp.concatenate([got[:1] + got[1:2], got[2:]])
        else:
            got = got[0::2] + got[1::2]
    return got[0].reshape(x.shape)


def split_dot(a, b):
    hi = lax.reduce_precision(a, exponent_bits=8, mantissa_bits=7)
    lo = a - hi
    b16 = b.astype(jnp.bfloat16)
    return (jnp.dot(hi.astype(jnp.bfloat16), b16, preferred_element_type=jnp.float32)
            + jnp.dot(lo.astype(jnp.bfloat16), b16, preferred_element_type=jnp.float32))


def body(visibilities, flags, taper, group_ids):
    _, local_chans, column_entries = visibilities.shape
    baselines = column_entries // 8
    n_chan = lax.axis_size("chan")
    channels = local_chans * n_chan
    shard_bl = baselines // n_chan
    shard_cols = shard_bl * 8
    times_all = lax.axis_size("tm")

    keep = (1 - flags[0]).astype(jnp.bfloat16).reshape(local_chans, n_chan, shard_bl)
    spread = (jnp.arange(shard_cols, dtype=jnp.int32)[None, :] // 8
              == jnp.arange(shard_bl, dtype=jnp.int32)[:, None]).astype(jnp.bfloat16)
    keep_cols = jnp.einsum("cjb,bl->jcl", keep, spread, preferred_element_type=jnp.float32)
    shaped = visibilities[0].reshape(local_chans, n_chan, shard_cols).transpose(1, 0, 2)
    tapered = (shaped.astype(jnp.float32) * (keep_cols * taper[None, :, None])).astype(jnp.bfloat16)

    member_full = (group_ids[:, None] == jnp.arange(G, dtype=jnp.int32)[None, :]).astype(jnp.bfloat16)
    member_full = member_full.reshape(n_chan, shard_bl, G)
    sums = jnp.einsum("jcbk,jbg->cgk", tapered.reshape(n_chan, local_chans, shard_bl, 8), member_full,
                      preferred_element_type=jnp.float32)
    sums = sums.reshape(local_chans, G * 8).T
    sums_hi = lax.reduce_precision(sums, exponent_bits=8, mantissa_bits=7)
    sums_lo = sums - sums_hi
    pad = shard_cols - 2 * local_chans
    extra_row = jnp.concatenate([
        sums_hi.astype(jnp.bfloat16),
        sums_lo.astype(jnp.bfloat16),
        jnp.zeros((n_chan, pad), jnp.bfloat16),
    ], axis=1)
    payload = jnp.concatenate([tapered, extra_row[:, None, :]], axis=1)
    got = lax.all_to_all(payload, "chan", 0, 0, tiled=True)
    turned = got[:, :local_chans, :].reshape(channels, shard_cols)
    col_parts = got[:, local_chans, :2 * local_chans].reshape(n_chan, 2, local_chans)
    col_parts = col_parts.transpose(0, 2, 1).reshape(channels, 2)

    cols = jnp.arange(shard_cols, dtype=jnp.int32)
    target = (cols % 2) * (shard_cols // 2) + cols // 2
    permute = (target[:, None] == cols[None, :]).astype(jnp.bfloat16)
    turned = jnp.dot(turned, permute, preferred_element_type=jnp.float32).astype(jnp.bfloat16)
    rhs = jnp.concatenate([turned, col_parts], axis=1)
    cos_tab, sin_tab = tables(channels, 128)
    cos_all = jnp.dot(cos_tab, rhs, preferred_element_type=jnp.float32)
    sin_all = jnp.dot(sin_tab, rhs, preferred_element_type=jnp.float32)
    cos_part, sin_part = cos_all[:, :shard_cols], sin_all[:, :shard_cols]
    col_cos = cos_all[:, shard_cols] + cos_all[:, shard_cols + 1]
    col_sin = sin_all[:, shard_cols] + sin_all[:, shard_cols + 1]

    me = lax.axis_index("chan")
    shard_groups = lax.dynamic_slice_in_dim(group_ids, me * shard_bl, shard_bl)
    member = (shard_groups[:, None] == jnp.arange(G, dtype=jnp.int32)[None, :]).astype(jnp.float32)
    eye_s = jnp.eye(4, dtype=jnp.float32)
    m_pow = (member[:, None, :, None] * eye_s[None, :, None, :]).reshape(shard_bl * 4, G * 4)
    half = shard_cols // 2
    real_part = cos_part[:, :half] + sin_part[:, half:]
    imag_part = cos_part[:, half:] - sin_part[:, :half]
    auto = split_dot(real_part * real_part + imag_part * imag_part, m_pow)

    own_d = channels // n_chan
    payload = jnp.concatenate([
        auto.reshape(n_chan, own_d * G * 4),
        col_cos.reshape(n_chan, own_d),
        col_sin.reshape(n_chan, own_d),
    ], axis=1)
    got = lax.all_to_all(payload, "chan", 0, 0, tiled=True)
    auto_own = jnp.sum(got[:, :own_d * G * 4], axis=0).reshape(own_d, G, 4)
    cs = got[:, own_d * G * 4:].reshape(G, 4, 2, 2, own_d)
    cs = cs.transpose(1, 0, 2, 3, 4)
    group_real = cs[:, :, 0, 0] + cs[:, :, 1, 1]
    group_imag = cs[:, :, 1, 0] - cs[:, :, 0, 1]
    cross = group_real * group_real + group_imag * group_imag - auto_own.transpose(2, 1, 0)
    cross = tm_sum(cross, times_all)

    member_all = (group_ids[None, :] == jnp.arange(G, dtype=jnp.int32)[:, None]).astype(jnp.float32)
    counts = jnp.sum(member_all, axis=1)
    pair_count = jnp.maximum(counts * (counts - 1.0), 1.0)
    norm = jnp.sqrt(pair_count * times_all)
    return cross / norm[None, :, None]


def solution(mesh):
    return jax.shard_map(
        body,
        mesh=mesh,
        in_specs=(P("tm", "chan", None), P("tm", "chan", None), P("chan"), P()),
        out_specs=P(None, None, "chan"),
        check_vma=False,
    )
```
